512 devices in a mesh: span: 128 (over z, x, y_hi), head: 4 (over y_lo, core).
Axes of the slice: x: 4, y: 4 (y_hi: 2, y_lo: 2; y = y_hi * 2 + y_lo), z: 16, core: 2. Of those that a mesh axis runs over, the one named last changes fastest.
Arguments:
- embedding_activity: bfloat16 [32768, 1024], P('span', 'head'), may hold values from -6 to 6
- common_lookup_projector: bfloat16 [1024, 1024], P(None, 'head'), may hold values from -0.1875 to 0.1875
- content_projector: bfloat16 [1024, 1024], P(None, 'head'), may hold values from -0.1875 to 0.1875
- final_projector: bfloat16 [1024, 1024], P('head'), may hold values from -3 to 3
- lane_sharpness: float32 [8], P('head'), may hold values from 4 to 16
- sorted_place_per_element: int32 [2, 32768], P(None, 'span'), may hold values from 0 to 32767, as said below
- element_per_sorted_place: int32 [2, 32768], P(None, 'span'), may hold values from 0 to 32767, as said below
Outputs:
- attended: bfloat16 [32768, 1024], P(('span', 'head'))
The draws below stay inside these ranges and needn't reach their ends.
Inputs may be any that keep to these rules, and one draw needn't show every extreme that they name: `sorted_place_per_element`: each round's row is a permutation of the tokens' sorted slots; slots d * 256 to (d + 1) * 256 - 1 belong to index d of span. In every round at most 4 tokens of one device's positions go to the slots of one device, and some device receives exactly 4 from one device. element_per_sorted_place[r] is the inverse permutation of sorted_place_per_element[r].
All inputs are finite; a program needn't handle non-finite values.
Results may differ from the reference program's by a relative error of at most 0.014.
Values may be sent and summed in bfloat16 or wider, within the bound.
No kernel may reach another device: no remote copies, remote signals or barrier semaphores. Data moves between devices by JAX's collectives and lax.ppermute only.
A program may use at most 64 MiB of HBM per device.

```python
import math
import jax
import jax.numpy as jnp
from jax import lax

D = 1024
ATTENTION_LANES = 8
HEAD_DIM = 128
BLOCK = 128
ROUNDS = 2
TOK_DEV = 256
SEQ = 32768
CAP = 4
HEADS_DEV = 2


def token_layout(key):
    n_dev = SEQ // TOK_DEV
    slot_ids = jnp.arange(TOK_DEV, dtype=jnp.int32)
    dev_ids = jnp.arange(n_dev, dtype=jnp.int32)
    rank_list = []
    token_list = []
    for round_no in range(ROUNDS):
        round_key = jax.random.fold_in(key, 7001 + round_no)
        split_keys = jax.random.split(round_key, 6)
        relabel_out = jax.random.permutation(split_keys[0], n_dev).astype(jnp.int32)
        relabel_in = jax.random.permutation(split_keys[1], n_dev).astype(jnp.int32)
        offsets = jax.random.permutation(split_keys[2], n_dev).astype(jnp.int32)
        first_half = jax.random.randint(split_keys[3], (n_dev // 2,), 0, CAP + 1, dtype=jnp.int32)
        first_half = first_half.at[0].set(CAP)
        group_sizes = jnp.stack([first_half, CAP - first_half], axis=1).reshape(n_dev)
        group_ends = jnp.cumsum(group_sizes)
        group_of = jnp.sum((slot_ids[:, None] >= group_ends[None, :]).astype(jnp.int32), axis=1)
        target = relabel_out[(relabel_in[:, None] + offsets[group_of][None, :]) % n_dev]
        base_rows = jnp.broadcast_to(slot_ids, (n_dev, TOK_DEV))
        local_pos = jax.random.permutation(split_keys[4], base_rows, axis=1, independent=True).astype(jnp.int32)
        target_slot = jax.random.permutation(split_keys[5], base_rows, axis=1, independent=True).astype(jnp.int32)
        rank_value = target * TOK_DEV + target_slot[target, jnp.broadcast_to(slot_ids, (n_dev, TOK_DEV))]
        token_ids = dev_ids[:, None] * TOK_DEV + local_pos
        ranks = jnp.zeros((SEQ,), jnp.int32).at[token_ids.reshape(-1)].set(rank_value.reshape(-1))
        holders = jnp.zeros((SEQ,), jnp.int32).at[rank_value.reshape(-1)].set(token_ids.reshape(-1))
        rank_list.append(ranks)
        token_list.append(holders)
    return (jnp.stack(rank_list), jnp.stack(token_list))


def draw_sorted_place_per_element(key, part):
    return token_layout(key)[0]


def draw_element_per_sorted_place(key, part):
    return token_layout(key)[1]


def block_levels(key, dims, cuts, low, largest):
    loudness = 1.0
    for position, shards_of in cuts:
        draws = jax.random.uniform(jax.random.fold_in(jax.random.fold_in(key, 6), position), (shards_of,), jnp.float32, low / len(cuts), largest / len(cuts))
        loudness = loudness * jnp.repeat(jnp.exp(draws), dims[position] // shards_of).reshape((-1,) + (1,) * (len(dims) - 1 - position))
    return loudness


def gaussian(own_key, shape, scale, bound, cuts=(), kind=jnp.bfloat16):
    factor_of = block_levels(own_key, shape, cuts, -0.22, 0.18) if cuts else 1.0
    array = jax.random.normal(own_key, shape, jnp.float32) * scale * factor_of
    return jnp.minimum(jnp.maximum(array, -bound), bound).astype(kind)


def setup_inputs(seed: int = 0) -> dict:
    streams_of = jax.random.split(jax.random.key(seed), 8)
    embedding_activity = gaussian(streams_of[0], (SEQ, D), 1.0, 6.0, ((0, 128), (1, 4)))
    common_lookup_projector = gaussian(streams_of[1], (D, ATTENTION_LANES * HEAD_DIM), D ** -0.5, 0.1875, ((1, 4),))
    content_projector = gaussian(streams_of[2], (D, ATTENTION_LANES * HEAD_DIM), D ** -0.5, 0.1875, ((1, 4),))
    final_projector = gaussian(streams_of[3], (ATTENTION_LANES * HEAD_DIM, D), (max(ATTENTION_LANES * HEAD_DIM // 256, 1)) ** -0.5, 3.0, ((0, 4),))
    lane_sharpness = jnp.clip(jnp.exp(math.log(16.0) - 1.3862944 * jax.random.uniform(streams_of[4], (ATTENTION_LANES,), jnp.float32) ** block_levels(streams_of[4], (ATTENTION_LANES,), ((0, 4),), -0.2, 0.2)), 4.0, 16.0)
    sorted_place_per_element = draw_sorted_place_per_element(jax.random.fold_in(streams_of[7], 71), 0)
    element_per_sorted_place = draw_element_per_sorted_place(jax.random.fold_in(streams_of[7], 71), 0)
    return {"embedding_activity": embedding_activity, "common_lookup_projector": common_lookup_projector, "content_projector": content_projector, "final_projector": final_projector, "lane_sharpness": lane_sharpness, "sorted_place_per_element": sorted_place_per_element, "element_per_sorted_place": element_per_sorted_place}


epsilon = 1e-05

def layer_norm(embedding_activity):
    content_embeddings = embedding_activity.astype(jnp.float32)
    row_mean = lax.optimization_barrier(jnp.mean(content_embeddings, axis=-1, keepdims=True))
    centred = content_embeddings - row_mean
    row_var = lax.optimization_barrier(jnp.mean(centred * centred, axis=-1, keepdims=True))
    return (centred * lax.rsqrt(row_var + epsilon)).astype(jnp.bfloat16)

def unit_rows(sorted_shared):
    content_embeddings = sorted_shared.reshape(-1, ATTENTION_LANES, HEAD_DIM).astype(jnp.float32)
    return (content_embeddings * lax.rsqrt(lax.optimization_barrier(jnp.sum(content_embeddings * content_embeddings, axis=-1, keepdims=True)) + 1e-06)).astype(jnp.bfloat16)

def grouped_similarity_mixing(unitlength_address_lines, content_projector_lines, lane_sharpness):
    per_group = TOK_DEV // BLOCK
    n_groups = SEQ // TOK_DEV
    keys_b = unitlength_address_lines.reshape(n_groups, per_group, BLOCK, ATTENTION_LANES, HEAD_DIM)
    vals_b = content_projector_lines.reshape(n_groups, per_group, BLOCK, ATTENTION_LANES, HEAD_DIM)
    prev_keys = jnp.roll(keys_b[:, -1], 1, axis=0)
    prev_vals = jnp.roll(vals_b[:, -1], 1, axis=0)
    allowed = jnp.arange(2 * BLOCK)[None, :] != jnp.arange(BLOCK)[:, None] + BLOCK

    def one_group(items):
        keys_g, vals_g, last_k, last_v = items
        key_rows = jnp.concatenate([jnp.concatenate([last_k[None], keys_g[:-1]], axis=0), keys_g], axis=1)
        val_rows = jnp.concatenate([jnp.concatenate([last_v[None], vals_g[:-1]], axis=0), vals_g], axis=1)
        similarity_energies = jnp.einsum('bqhd,bkhd->bhqk', keys_g.astype(jnp.float32), key_rows.astype(jnp.float32), precision=lax.Precision.HIGHEST)
        similarity_energies = similarity_energies * lane_sharpness.astype(jnp.float32)[None, :, None, None]
        exp_scores = jnp.where(allowed, jnp.exp(similarity_energies), jnp.zeros_like(similarity_energies))
        softmax_normalizers = lax.optimization_barrier(jnp.sum(exp_scores, axis=-1))
        weights = (exp_scores / softmax_normalizers[..., None]).astype(jnp.bfloat16)
        blended_result = jnp.einsum('bhqk,bkhd->bqhd', weights.astype(jnp.float32), val_rows.astype(jnp.float32), precision=lax.Precision.HIGHEST).astype(jnp.bfloat16)
        return (blended_result, jnp.transpose(softmax_normalizers, (0, 2, 1)))
    blended_result, softmax_normalizers = lax.map(one_group, (keys_b, vals_b, prev_keys, prev_vals))
    return (blended_result.reshape(SEQ, ATTENTION_LANES * HEAD_DIM), softmax_normalizers.reshape(SEQ, ATTENTION_LANES))

def reference(embedding_activity, common_lookup_projector, content_projector, final_projector, lane_sharpness, sorted_place_per_element, element_per_sorted_place):
    normed = layer_norm(embedding_activity)
    shared = jnp.dot(normed, common_lookup_projector, preferred_element_type=jnp.float32).astype(jnp.bfloat16)
    content_embeddings = jnp.dot(normed, content_projector, preferred_element_type=jnp.float32).astype(jnp.bfloat16)
    outs_list = []
    totals_list = []
    for round_no in range(ROUNDS):
        gathered_entries = element_per_sorted_place[round_no].astype(jnp.int32)
        unitlength_address_lines = unit_rows(shared[gathered_entries])
        blended_result, softmax_normalizers = grouped_similarity_mixing(unitlength_address_lines, content_embeddings[gathered_entries], lane_sharpness)
        back = sorted_place_per_element[round_no].astype(jnp.int32)
        outs_list.append(blended_result[back])
        totals_list.append(softmax_normalizers[back])
    token_out = jnp.stack(outs_list)
    token_totals = jnp.stack(totals_list)
    n_groups = SEQ // TOK_DEV
    out_groups = jnp.transpose(token_out.reshape(ROUNDS, n_groups, TOK_DEV, ATTENTION_LANES * HEAD_DIM), (1, 0, 2, 3))
    total_groups = jnp.transpose(token_totals.reshape(ROUNDS, n_groups, TOK_DEV, ATTENTION_LANES), (1, 0, 2, 3))
    group_cols = HEADS_DEV * HEAD_DIM

    def project(items):
        round_rows, round_totals = items
        round_share = round_totals / lax.optimization_barrier(jnp.sum(round_totals, axis=0))
        spread = round_rows.reshape(ROUNDS, TOK_DEV, ATTENTION_LANES, HEAD_DIM).astype(jnp.float32)
        combined = lax.optimization_barrier(jnp.sum(round_share[..., None] * spread, axis=0)).astype(jnp.bfloat16)
        combined = combined.reshape(TOK_DEV, ATTENTION_LANES * HEAD_DIM)
        summed = jnp.zeros((TOK_DEV, D), jnp.float32)
        for head_group in range(ATTENTION_LANES // HEADS_DEV):
            lower = head_group * group_cols
            partial_out = jnp.dot(combined[:, lower:lower + group_cols], final_projector[lower:lower + group_cols], preferred_element_type=jnp.float32)
            summed = summed + partial_out.astype(jnp.bfloat16).astype(jnp.float32)
        return summed.astype(jnp.bfloat16)
    attended = lax.map(project, (out_groups, total_groups))
    return attended.reshape(SEQ, D)
```

```python
import jax
import jax.numpy as jnp
from jax import lax
from jax.sharding import PartitionSpec as P

HEAD_DIM = 128
BLOCK = 128


epsilon = 1e-05


def passed_along(block, axis, distance):
    devices = range(lax.axis_size(axis))
    route = [((i - distance) % len(devices), i) for i in devices]
    return lax.ppermute(block, axis, route)


def layer_norm(embedding_activity):
    content_embeddings = embedding_activity.astype(jnp.float32)
    row_mean = jnp.mean(content_embeddings, axis=-1, keepdims=True)
    centred = content_embeddings - row_mean
    row_var = jnp.mean(centred * centred, axis=-1, keepdims=True)
    return (centred * lax.rsqrt(row_var + epsilon)).astype(jnp.bfloat16)


def rank_within_group(group, order):
    same = group[:, :, None] == group[:, None, :]
    earlier = order[:, None, :] < order[:, :, None]
    return jnp.sum((same & earlier).astype(jnp.int32), axis=2)


def one_hot_rows(index, count):
    return (index[:, :, None] == jnp.arange(count, dtype=jnp.int32)[None, None, :]).astype(
        jnp.bfloat16
    )


def shards(
    embedding_activity,
    common_lookup_projector,
    content_projector,
    final_projector,
    lane_sharpness,
    sorted_place_per_element,
    element_per_sorted_place,
):
    n_dev = lax.axis_size("span")
    rows_here = embedding_activity.shape[0]
    capacity = 2 * rows_here // n_dev
    n_rounds = sorted_place_per_element.shape[0]
    per_peer = n_rounds * capacity
    buffer_rows = n_dev * per_peer
    head_cols = common_lookup_projector.shape[1]
    heads_here = head_cols // HEAD_DIM
    blocks_here = rows_here // BLOCK
    round_ids = jnp.arange(n_rounds, dtype=jnp.int32)[:, None]
    local_ids = jnp.broadcast_to(
        jnp.arange(rows_here, dtype=jnp.int32)[None, :], (n_rounds, rows_here)
    )

    target = sorted_place_per_element // rows_here
    send_rank = rank_within_group(target, local_ids)
    send_row = target * per_peer + round_ids * capacity + send_rank
    send_hot = one_hot_rows(send_row, buffer_rows)

    source = element_per_sorted_place // rows_here
    within = element_per_sorted_place % rows_here
    recv_rank = rank_within_group(source, within)
    recv_row = source * per_peer + round_ids * capacity + recv_rank
    recv_hot = one_hot_rows(recv_row, buffer_rows)

    full_rows = lax.all_gather(embedding_activity, "head", axis=1, tiled=True)
    normed = layer_norm(full_rows)
    joined = jnp.concatenate([common_lookup_projector, content_projector], axis=1)
    both = jnp.dot(normed, joined, preferred_element_type=jnp.float32).astype(jnp.bfloat16)

    outgoing = jnp.einsum(
        "rtq,tw->qw", send_hot, both, preferred_element_type=jnp.float32
    ).astype(jnp.bfloat16)
    incoming = lax.all_to_all(outgoing, "span", split_axis=0, concat_axis=0, tiled=True)
    arrived = jnp.einsum(
        "rsq,qw->rsw", recv_hot, incoming, preferred_element_type=jnp.float32
    ).astype(jnp.bfloat16)

    sorted_shared = arrived[:, :, :head_cols]
    sorted_values = arrived[:, :, head_cols:]
    spread = sorted_shared.reshape(n_rounds, rows_here, heads_here, HEAD_DIM).astype(jnp.float32)
    unitlength_address_lines = (
        spread * lax.rsqrt(jnp.sum(spread * spread, axis=-1, keepdims=True) + 1e-06)
    ).astype(jnp.bfloat16)
    unitlength_address_lines = unitlength_address_lines.reshape(n_rounds, rows_here, head_cols)
    last_block = jnp.concatenate(
        [unitlength_address_lines[:, rows_here - BLOCK :], sorted_values[:, rows_here - BLOCK :]],
        axis=2,
    )
    prior_block = passed_along(last_block, "span", 1)
    keys_cur = unitlength_address_lines.reshape(n_rounds, blocks_here, BLOCK, head_cols)
    vals_cur = sorted_values.reshape(n_rounds, blocks_here, BLOCK, head_cols)
    keys_prev = jnp.concatenate([prior_block[:, None, :, :head_cols], keys_cur[:, :-1]], axis=1)
    vals_prev = jnp.concatenate([prior_block[:, None, :, head_cols:], vals_cur[:, :-1]], axis=1)
    key_rows = jnp.concatenate([keys_prev, keys_cur], axis=2).reshape(
        n_rounds, blocks_here, 2 * BLOCK, heads_here, HEAD_DIM
    )
    content_projector_lines = jnp.concatenate([vals_prev, vals_cur], axis=2).reshape(
        n_rounds, blocks_here, 2 * BLOCK, heads_here, HEAD_DIM
    )
    queries = keys_cur.reshape(n_rounds, blocks_here, BLOCK, heads_here, HEAD_DIM)
    similarity_energies = jnp.einsum(
        "rbqhd,rbkhd->rbhqk", queries, key_rows, preferred_element_type=jnp.float32
    )
    similarity_energies = similarity_energies * lane_sharpness[None, None, :, None, None]
    allowed = jnp.arange(2 * BLOCK)[None, :] != jnp.arange(BLOCK)[:, None] + BLOCK
    exp_scores = jnp.where(allowed, jnp.exp(similarity_energies), 0.0)
    row_totals = jnp.sum(exp_scores, axis=-1)
    weights = (exp_scores / row_totals[..., None]).astype(jnp.bfloat16)
    results = jnp.einsum(
        "rbhqk,rbkhd->rbqhd", weights, content_projector_lines, preferred_element_type=jnp.float32
    )
    results = results.astype(jnp.bfloat16).reshape(n_rounds, rows_here, head_cols)
    slot_totals = jnp.transpose(row_totals, (0, 1, 3, 2)).reshape(n_rounds, rows_here, heads_here)
    totals_high = slot_totals.astype(jnp.bfloat16)
    totals_low = (slot_totals - totals_high.astype(jnp.float32)).astype(jnp.bfloat16)
    back_payload = jnp.concatenate([results, totals_high, totals_low], axis=2)

    back = jnp.einsum(
        "rsq,rsw->qw", recv_hot, back_payload, preferred_element_type=jnp.float32
    ).astype(jnp.bfloat16)
    home = lax.all_to_all(back, "span", split_axis=0, concat_axis=0, tiled=True)
    token_all = jnp.einsum("rtq,qw->rtw", send_hot, home, preferred_element_type=jnp.float32)
    token_rows = token_all[:, :, :head_cols]
    token_totals = (
        token_all[:, :, head_cols : head_cols + heads_here]
        + token_all[:, :, head_cols + heads_here : head_cols + 2 * heads_here]
    )
    round_share = token_totals / jnp.sum(token_totals, axis=0)
    token_spread = token_rows.reshape(n_rounds, rows_here, heads_here, HEAD_DIM)
    combined = jnp.sum(round_share[..., None] * token_spread, axis=0).astype(jnp.bfloat16)
    combined = combined.reshape(rows_here, head_cols)
    return lax.psum_scatter(
        jnp.dot(combined, final_projector, preferred_element_type=jnp.float32).astype(jnp.bfloat16),
        "head",
        scatter_dimension=0,
        tiled=True,
    )


def solution(mesh):
    placed = (
        P("span", "head"),
        P(None, "head"),
        P(None, "head"),
        P("head", None),
        P("head"),
        P(None, "span"),
        P(None, "span"),
    )
    return jax.shard_map(
        shards, mesh=mesh, in_specs=placed, out_specs=P(("span", "head"), None), check_vma=False
    )
```

```python
import jax
import jax.numpy as jnp
from jax import lax
from jax.sharding import PartitionSpec as P

HEAD_DIM = 128
BLOCK = 128


epsilon = 1e-05


def passed_along(block, axis, distance):
    devices = range(lax.axis_size(axis))
    route = [((i - distance) % len(devices), i) for i in devices]
    return lax.ppermute(block, axis, route)


def layer_norm(embedding_activity):
    content_embeddings = embedding_activity.astype(jnp.float32)
    row_mean = jnp.mean(content_embeddings, axis=-1, keepdims=True)
    centred = content_embeddings - row_mean
    row_var = jnp.mean(centred * centred, axis=-1, keepdims=True)
    return (centred * lax.rsqrt(row_var + epsilon)).astype(jnp.bfloat16)


def rank_within_group(group, order):
    same = group[:, :, None] == group[:, None, :]
    earlier = order[:, None, :] < order[:, :, None]
    return jnp.sum((same & earlier).astype(jnp.int32), axis=2)


def one_hot_rows(index, count):
    return (index[:, :, None] == jnp.arange(count, dtype=jnp.int32)[None, None, :]).astype(
        jnp.bfloat16
    )


def shards(
    embedding_activity,
    common_lookup_projector,
    content_projector,
    final_projector,
    lane_sharpness,
    sorted_place_per_element,
    element_per_sorted_place,
):
    n_dev = lax.axis_size("span")
    rows_here = embedding_activity.shape[0]
    capacity = 2 * rows_here // n_dev
    n_rounds = sorted_place_per_element.shape[0]
    per_peer = n_rounds * capacity
    buffer_rows = n_dev * per_peer
    head_cols = common_lookup_projector.shape[1]
    heads_here = head_cols // HEAD_DIM
    blocks_here = rows_here // BLOCK
    round_ids = jnp.arange(n_rounds, dtype=jnp.int32)[:, None]
    local_ids = jnp.broadcast_to(
        jnp.arange(rows_here, dtype=jnp.int32)[None, :], (n_rounds, rows_here)
    )

    target = sorted_place_per_element // rows_here
    send_rank = rank_within_group(target, local_ids)
    send_row = target * per_peer + round_ids * capacity + send_rank
    send_hot = one_hot_rows(send_row, buffer_rows)

    source = element_per_sorted_place // rows_here
    within = element_per_sorted_place % rows_here
    recv_rank = rank_within_group(source, within)
    recv_row = source * per_peer + round_ids * capacity + recv_rank
    recv_hot = one_hot_rows(recv_row, buffer_rows)

    outgoing = jnp.einsum(
        "rtq,tf->qf", send_hot, embedding_activity, preferred_element_type=jnp.float32
    ).astype(jnp.bfloat16)
    incoming = lax.all_to_all(outgoing, "span", split_axis=0, concat_axis=0, tiled=True)
    arrived = jnp.einsum(
        "rsq,qf->rsf", recv_hot, incoming, preferred_element_type=jnp.float32
    ).astype(jnp.bfloat16)
    prior_block = passed_along(arrived[:, rows_here - BLOCK :], "span", 1)
    with_prior = jnp.concatenate([prior_block, arrived], axis=1)
    full_rows = lax.all_gather(with_prior, "head", axis=2, tiled=True)
    normed = layer_norm(full_rows)
    joined = jnp.concatenate([common_lookup_projector, content_projector], axis=1)
    both = jnp.einsum(
        "rsf,fw->rsw", normed, joined, preferred_element_type=jnp.float32
    ).astype(jnp.bfloat16)
    span_rows = rows_here + BLOCK
    sorted_shared = both[:, :, :head_cols]
    sorted_values = both[:, :, head_cols:]
    spread = sorted_shared.reshape(n_rounds, span_rows, heads_here, HEAD_DIM).astype(jnp.float32)
    unitlength_address_lines = (
        spread * lax.rsqrt(jnp.sum(spread * spread, axis=-1, keepdims=True) + 1e-06)
    ).astype(jnp.bfloat16)
    unitlength_address_lines = unitlength_address_lines.reshape(n_rounds, span_rows, head_cols)
    keys_cur = unitlength_address_lines[:, BLOCK:].reshape(n_rounds, blocks_here, BLOCK, head_cols)
    key_rows = jnp.stack(
        [unitlength_address_lines[:, b * BLOCK : b * BLOCK + 2 * BLOCK] for b in range(blocks_here)],
        axis=1,
    ).reshape(n_rounds, blocks_here, 2 * BLOCK, heads_here, HEAD_DIM)
    content_projector_lines = jnp.stack(
        [sorted_values[:, b * BLOCK : b * BLOCK + 2 * BLOCK] for b in range(blocks_here)], axis=1
    ).reshape(n_rounds, blocks_here, 2 * BLOCK, heads_here, HEAD_DIM)
    queries = keys_cur.reshape(n_rounds, blocks_here, BLOCK, heads_here, HEAD_DIM)
    similarity_energies = jnp.einsum(
        "rbqhd,rbkhd->rbhqk", queries, key_rows, preferred_element_type=jnp.float32
    )
    similarity_energies = similarity_energies * lane_sharpness[None, None, :, None, None]
    allowed = jnp.arange(2 * BLOCK)[None, :] != jnp.arange(BLOCK)[:, None] + BLOCK
    exp_scores = jnp.where(allowed, jnp.exp(similarity_energies), 0.0)
    row_totals = jnp.sum(exp_scores, axis=-1)
    weights = (exp_scores / row_totals[..., None]).astype(jnp.bfloat16)
    results = jnp.einsum(
        "rbhqk,rbkhd->rbqhd", weights, content_projector_lines, preferred_element_type=jnp.float32
    )
    results = results.astype(jnp.bfloat16).reshape(n_rounds, rows_here, head_cols)
    slot_totals = jnp.transpose(row_totals, (0, 1, 3, 2)).reshape(n_rounds, rows_here, heads_here)
    totals_high = slot_totals.astype(jnp.bfloat16)
    totals_low = (slot_totals - totals_high.astype(jnp.float32)).astype(jnp.bfloat16)
    back_payload = jnp.concatenate([results, totals_high, totals_low], axis=2)

    back = jnp.einsum(
        "rsq,rsw->qw", recv_hot, back_payload, preferred_element_type=jnp.float32
    ).astype(jnp.bfloat16)
    home = lax.all_to_all(back, "span", split_axis=0, concat_axis=0, tiled=True)
    token_all = jnp.einsum("rtq,qw->rtw", send_hot, home, preferred_element_type=jnp.float32)
    token_rows = token_all[:, :, :head_cols]
    token_totals = (
        token_all[:, :, head_cols : head_cols + heads_here]
        + token_all[:, :, head_cols + heads_here : head_cols + 2 * heads_here]
    )
    round_share = token_totals / jnp.sum(token_totals, axis=0)
    token_spread = token_rows.reshape(n_rounds, rows_here, heads_here, HEAD_DIM)
    combined = jnp.sum(round_share[..., None] * token_spread, axis=0).astype(jnp.bfloat16)
    combined = combined.reshape(rows_here, head_cols)
    return lax.psum_scatter(
        jnp.dot(combined, final_projector, preferred_element_type=jnp.float32).astype(jnp.bfloat16),
        "head",
        scatter_dimension=0,
        tiled=True,
    )


def solution(mesh):
    placed = (
        P("span", "head"),
        P(None, "head"),
        P(None, "head"),
        P("head", None),
        P("head"),
        P(None, "span"),
        P(None, "span"),
    )
    return jax.shard_map(
        shards, mesh=mesh, in_specs=placed, out_specs=P(("span", "head"), None), check_vma=False
    )
```

```python
import jax
import jax.numpy as jnp
from jax import lax
from jax.sharding import Mesh, PartitionSpec as P

HEAD_DIM = 128
BLOCK = 128


epsilon = 1e-05

SPAN_FACTORS = (16, 4, 2)
SPAN_AXES = ("span_z", "span_x", "span_y")


def staged_all_to_all(rows, axes):
    sizes = tuple(lax.axis_size(axis) for axis in axes)
    count = 1
    for size in sizes:
        count *= size
    per_peer = rows.shape[0] // count
    staged = rows.reshape(sizes + (per_peer,) + rows.shape[1:])
    for place, axis in enumerate(axes):
        staged = lax.all_to_all(staged, axis, split_axis=place, concat_axis=place, tiled=True)
    return staged.reshape(rows.shape)


def passed_along(block, axis, distance):
    devices = range(lax.axis_size(axis))
    route = [((i - distance) % len(devices), i) for i in devices]
    return lax.ppermute(block, axis, route)


def layer_norm(embedding_activity):
    content_embeddings = embedding_activity.astype(jnp.float32)
    row_mean = jnp.mean(content_embeddings, axis=-1, keepdims=True)
    centred = content_embeddings - row_mean
    row_var = jnp.mean(centred * centred, axis=-1, keepdims=True)
    return (centred * lax.rsqrt(row_var + epsilon)).astype(jnp.bfloat16)


def rank_within_group(group, order):
    same = group[:, :, None] == group[:, None, :]
    earlier = order[:, None, :] < order[:, :, None]
    return jnp.sum((same & earlier).astype(jnp.int32), axis=2)


def one_hot_rows(index, count):
    return (index[:, :, None] == jnp.arange(count, dtype=jnp.int32)[None, None, :]).astype(
        jnp.bfloat16
    )


def shards(
    embedding_activity,
    common_lookup_projector,
    content_projector,
    final_projector,
    lane_sharpness,
    sorted_place_per_element,
    element_per_sorted_place,
):
    n_dev = lax.axis_size(SPAN_AXES)
    rows_here = embedding_activity.shape[0]
    capacity = 2 * rows_here // n_dev
    n_rounds = sorted_place_per_element.shape[0]
    per_peer = n_rounds * capacity
    buffer_rows = n_dev * per_peer
    head_cols = common_lookup_projector.shape[1]
    heads_here = head_cols // HEAD_DIM
    blocks_here = rows_here // BLOCK
    round_ids = jnp.arange(n_rounds, dtype=jnp.int32)[:, None]
    local_ids = jnp.broadcast_to(
        jnp.arange(rows_here, dtype=jnp.int32)[None, :], (n_rounds, rows_here)
    )

    target = sorted_place_per_element // rows_here
    send_rank = rank_within_group(target, local_ids)
    send_row = target * per_peer + round_ids * capacity + send_rank
    send_hot = one_hot_rows(send_row, buffer_rows)

    source = element_per_sorted_place // rows_here
    within = element_per_sorted_place % rows_here
    recv_rank = rank_within_group(source, within)
    recv_row = source * per_peer + round_ids * capacity + recv_rank
    recv_hot = one_hot_rows(recv_row, buffer_rows)

    outgoing = jnp.einsum(
        "rtq,tf->qf", send_hot, embedding_activity, preferred_element_type=jnp.float32
    ).astype(jnp.bfloat16)
    incoming = staged_all_to_all(outgoing, SPAN_AXES)
    arrived = jnp.einsum(
        "rsq,qf->rsf", recv_hot, incoming, preferred_element_type=jnp.float32
    ).astype(jnp.bfloat16)
    prior_block = passed_along(arrived[:, rows_here - BLOCK :], SPAN_AXES, 1)
    with_prior = jnp.concatenate([prior_block, arrived], axis=1)
    full_rows = lax.all_gather(with_prior, "head", axis=2, tiled=True)
    normed = layer_norm(full_rows)
    joined = jnp.concatenate([common_lookup_projector, content_projector], axis=1)
    both = jnp.einsum(
        "rsf,fw->rsw", normed, joined, preferred_element_type=jnp.float32
    ).astype(jnp.bfloat16)
    span_rows = rows_here + BLOCK
    sorted_shared = both[:, :, :head_cols]
    sorted_values = both[:, :, head_cols:]
    spread = sorted_shared.reshape(n_rounds, span_rows, heads_here, HEAD_DIM).astype(jnp.float32)
    unitlength_address_lines = (
        spread * lax.rsqrt(jnp.sum(spread * spread, axis=-1, keepdims=True) + 1e-06)
    ).astype(jnp.bfloat16)
    unitlength_address_lines = unitlength_address_lines.reshape(n_rounds, span_rows, head_cols)
    keys_cur = unitlength_address_lines[:, BLOCK:].reshape(n_rounds, blocks_here, BLOCK, head_cols)
    key_rows = jnp.stack(
        [unitlength_address_lines[:, b * BLOCK : b * BLOCK + 2 * BLOCK] for b in range(blocks_here)],
        axis=1,
    ).reshape(n_rounds, blocks_here, 2 * BLOCK, heads_here, HEAD_DIM)
    content_projector_lines = jnp.stack(
        [sorted_values[:, b * BLOCK : b * BLOCK + 2 * BLOCK] for b in range(blocks_here)], axis=1
    ).reshape(n_rounds, blocks_here, 2 * BLOCK, heads_here, HEAD_DIM)
    queries = keys_cur.reshape(n_rounds, blocks_here, BLOCK, heads_here, HEAD_DIM)
    similarity_energies = jnp.einsum(
        "rbqhd,rbkhd->rbhqk", queries, key_rows, preferred_element_type=jnp.float32
    )
    similarity_energies = similarity_energies * lane_sharpness[None, None, :, None, None]
    allowed = jnp.arange(2 * BLOCK)[None, :] != jnp.arange(BLOCK)[:, None] + BLOCK
    exp_scores = jnp.where(allowed, jnp.exp(similarity_energies), 0.0)
    row_totals = jnp.sum(exp_scores, axis=-1)
    weights = (exp_scores / row_totals[..., None]).astype(jnp.bfloat16)
    results = jnp.einsum(
        "rbhqk,rbkhd->rbqhd", weights, content_projector_lines, preferred_element_type=jnp.float32
    )
    results = results.astype(jnp.bfloat16).reshape(n_rounds, rows_here, head_cols)
    slot_totals = jnp.transpose(row_totals, (0, 1, 3, 2)).reshape(n_rounds, rows_here, heads_here)
    totals_high = slot_totals.astype(jnp.bfloat16)
    totals_low = (slot_totals - totals_high.astype(jnp.float32)).astype(jnp.bfloat16)
    back_payload = jnp.concatenate([results, totals_high, totals_low], axis=2)

    back = jnp.einsum(
        "rsq,rsw->qw", recv_hot, back_payload, preferred_element_type=jnp.float32
    ).astype(jnp.bfloat16)
    home = staged_all_to_all(back, SPAN_AXES)
    token_all = jnp.einsum("rtq,qw->rtw", send_hot, home, preferred_element_type=jnp.float32)
    token_rows = token_all[:, :, :head_cols]
    token_totals = (
        token_all[:, :, head_cols : head_cols + heads_here]
        + token_all[:, :, head_cols + heads_here : head_cols + 2 * heads_here]
    )
    round_share = token_totals / jnp.sum(token_totals, axis=0)
    token_spread = token_rows.reshape(n_rounds, rows_here, heads_here, HEAD_DIM)
    combined = jnp.sum(round_share[..., None] * token_spread, axis=0).astype(jnp.bfloat16)
    combined = combined.reshape(rows_here, head_cols)
    return lax.psum_scatter(
        jnp.dot(combined, final_projector, preferred_element_type=jnp.float32).astype(jnp.bfloat16),
        "head",
        scatter_dimension=0,
        tiled=True,
    )


def solution(mesh):
    assert mesh.shape["span"] == SPAN_FACTORS[0] * SPAN_FACTORS[1] * SPAN_FACTORS[2]
    split_mesh = Mesh(
        mesh.devices.reshape(SPAN_FACTORS + (mesh.shape["head"],)), SPAN_AXES + ("head",)
    )
    placed = (
        P(SPAN_AXES, "head"),
        P(None, "head"),
        P(None, "head"),
        P("head", None),
        P("head"),
        P(None, SPAN_AXES),
        P(None, SPAN_AXES),
    )
    return jax.shard_map(
        shards,
        mesh=split_mesh,
        in_specs=placed,
        out_specs=P(SPAN_AXES + ("head",), None),
        check_vma=False,
    )
```

```python
import jax
import jax.numpy as jnp
from jax import lax
from jax.sharding import PartitionSpec as P

HEAD_DIM = 128
BLOCK = 128


epsilon = 1e-05


def passed_along(block, axis, distance):
    devices = range(lax.axis_size(axis))
    route = [((i - distance) % len(devices), i) for i in devices]
    return lax.ppermute(block, axis, route)


def layer_norm(embedding_activity):
    content_embeddings = embedding_activity.astype(jnp.float32)
    row_mean = jnp.mean(content_embeddings, axis=-1, keepdims=True)
    centred = content_embeddings - row_mean
    row_var = jnp.mean(centred * centred, axis=-1, keepdims=True)
    return (centred * lax.rsqrt(row_var + epsilon)).astype(jnp.bfloat16)


def rank_within_group(group, order):
    same = group[:, :, None] == group[:, None, :]
    earlier = order[:, None, :] < order[:, :, None]
    return jnp.sum((same & earlier).astype(jnp.int32), axis=2)


def one_hot_rows(index, count):
    return (index[:, :, None] == jnp.arange(count, dtype=jnp.int32)[None, None, :]).astype(
        jnp.bfloat16
    )


def shards(
    embedding_activity,
    common_lookup_projector,
    content_projector,
    final_projector,
    lane_sharpness,
    sorted_place_per_element,
    element_per_sorted_place,
):
    n_dev = lax.axis_size("span")
    rows_here = embedding_activity.shape[0]
    capacity = 2 * rows_here // n_dev
    n_rounds = sorted_place_per_element.shape[0]
    per_peer = n_rounds * capacity
    buffer_rows = n_dev * per_peer
    head_cols = common_lookup_projector.shape[1]
    heads_here = head_cols // HEAD_DIM
    blocks_here = rows_here // BLOCK
    round_ids = jnp.arange(n_rounds, dtype=jnp.int32)[:, None]
    local_ids = jnp.broadcast_to(
        jnp.arange(rows_here, dtype=jnp.int32)[None, :], (n_rounds, rows_here)
    )

    target = sorted_place_per_element // rows_here
    send_rank = rank_within_group(target, local_ids)
    send_row = target * per_peer + round_ids * capacity + send_rank
    send_hot = one_hot_rows(send_row, buffer_rows)

    source = element_per_sorted_place // rows_here
    within = element_per_sorted_place % rows_here
    recv_rank = rank_within_group(source, within)
    recv_row = source * per_peer + round_ids * capacity + recv_rank
    recv_hot = one_hot_rows(recv_row, buffer_rows)

    outgoing = jnp.einsum(
        "rtq,tf->qf", send_hot, embedding_activity, preferred_element_type=jnp.float32
    ).astype(jnp.bfloat16)
    incoming = lax.all_to_all(outgoing, "span", split_axis=0, concat_axis=0, tiled=True)
    arrived = jnp.einsum(
        "rsq,qf->rsf", recv_hot, incoming, preferred_element_type=jnp.float32
    ).astype(jnp.bfloat16)
    prior_block = passed_along(arrived[:, rows_here - BLOCK :], "span", 1)
    with_prior = jnp.concatenate([prior_block, arrived], axis=1)
    full_rows = lax.all_gather(with_prior, "head", axis=2, tiled=True)
    normed = layer_norm(full_rows)
    joined = jnp.concatenate([common_lookup_projector, content_projector], axis=1)
    both = jnp.einsum(
        "rsf,fw->rsw", normed, joined, preferred_element_type=jnp.float32
    ).astype(jnp.bfloat16)
    span_rows = rows_here + BLOCK
    sorted_shared = both[:, :, :head_cols]
    sorted_values = both[:, :, head_cols:]
    spread = sorted_shared.reshape(n_rounds, span_rows, heads_here, HEAD_DIM).astype(jnp.float32)
    unitlength_address_lines = (
        spread * lax.rsqrt(jnp.sum(spread * spread, axis=-1, keepdims=True) + 1e-06)
    ).astype(jnp.bfloat16)
    unitlength_address_lines = unitlength_address_lines.reshape(n_rounds, span_rows, head_cols)
    keys_cur = unitlength_address_lines[:, BLOCK:].reshape(n_rounds, blocks_here, BLOCK, head_cols)
    key_rows = jnp.stack(
        [unitlength_address_lines[:, b * BLOCK : b * BLOCK + 2 * BLOCK] for b in range(blocks_here)],
        axis=1,
    ).reshape(n_rounds, blocks_here, 2 * BLOCK, heads_here, HEAD_DIM)
    content_projector_lines = jnp.stack(
        [sorted_values[:, b * BLOCK : b * BLOCK + 2 * BLOCK] for b in range(blocks_here)], axis=1
    ).reshape(n_rounds, blocks_here, 2 * BLOCK, heads_here, HEAD_DIM)
    queries = keys_cur.reshape(n_rounds, blocks_here, BLOCK, heads_here, HEAD_DIM)
    similarity_energies = jnp.einsum(
        "rbqhd,rbkhd->rbhqk", queries, key_rows, preferred_element_type=jnp.float32
    )
    similarity_energies = similarity_energies * lane_sharpness[None, None, :, None, None]
    allowed = jnp.arange(2 * BLOCK)[None, :] != jnp.arange(BLOCK)[:, None] + BLOCK
    exp_scores = jnp.where(allowed, jnp.exp(similarity_energies), 0.0)
    row_totals = jnp.sum(exp_scores, axis=-1)
    weights = (exp_scores / row_totals[..., None]).astype(jnp.bfloat16)
    results = jnp.einsum(
        "rbhqk,rbkhd->rbqhd", weights, content_projector_lines, preferred_element_type=jnp.float32
    )
    results = results.astype(jnp.bfloat16).reshape(n_rounds, rows_here, head_cols)
    slot_totals = jnp.transpose(row_totals, (0, 1, 3, 2)).reshape(n_rounds, rows_here, heads_here)
    totals_high = slot_totals.astype(jnp.bfloat16)
    totals_low = (slot_totals - totals_high.astype(jnp.float32)).astype(jnp.bfloat16)
    back_payload = jnp.concatenate([results, totals_high, totals_low], axis=2)

    back = jnp.einsum(
        "rsq,rsw->qw", recv_hot, back_payload, preferred_element_type=jnp.float32
    ).astype(jnp.bfloat16)
    back_width = back.shape[1]
    home = lax.all_to_all(
        back.reshape(n_dev, per_peer * back_width), "span", split_axis=0, concat_axis=0, tiled=True
    ).reshape(buffer_rows, back_width)
    token_all = jnp.einsum("rtq,qw->rtw", send_hot, home, preferred_element_type=jnp.float32)
    token_rows = token_all[:, :, :head_cols]
    token_totals = (
        token_all[:, :, head_cols : head_cols + heads_here]
        + token_all[:, :, head_cols + heads_here : head_cols + 2 * heads_here]
    )
    round_share = token_totals / jnp.sum(token_totals, axis=0)
    token_spread = token_rows.reshape(n_rounds, rows_here, heads_here, HEAD_DIM)
    combined = jnp.sum(round_share[..., None] * token_spread, axis=0).astype(jnp.bfloat16)
    combined = combined.reshape(rows_here, head_cols)
    return lax.psum_scatter(
        jnp.dot(combined, final_projector, preferred_element_type=jnp.float32).astype(jnp.bfloat16),
        "head",
        scatter_dimension=0,
        tiled=True,
    )


def solution(mesh):
    placed = (
        P("span", "head"),
        P(None, "head"),
        P(None, "head"),
        P("head", None),
        P("head"),
        P(None, "span"),
        P(None, "span"),
    )
    return jax.shard_map(
        shards, mesh=mesh, in_specs=placed, out_specs=P(("span", "head"), None), check_vma=False
    )
```

```python
import jax
import jax.numpy as jnp
from jax import lax
from jax.sharding import PartitionSpec as P

HEAD_DIM = 128
BLOCK = 128


epsilon = 1e-05


def passed_along(block, axis, distance):
    devices = range(lax.axis_size(axis))
    route = [((i - distance) % len(devices), i) for i in devices]
    return lax.ppermute(block, axis, route)


def layer_norm(embedding_activity):
    content_embeddings = embedding_activity.astype(jnp.float32)
    row_mean = jnp.mean(content_embeddings, axis=-1, keepdims=True)
    centred = content_embeddings - row_mean
    row_var = jnp.mean(centred * centred, axis=-1, keepdims=True)
    return (centred * lax.rsqrt(row_var + epsilon)).astype(jnp.bfloat16)


def rank_within_group(group, order):
    same = group[:, :, None] == group[:, None, :]
    earlier = order[:, None, :] < order[:, :, None]
    return jnp.sum((same & earlier).astype(jnp.int32), axis=2)


def one_hot_rows(index, count):
    return (index[:, :, None] == jnp.arange(count, dtype=jnp.int32)[None, None, :]).astype(
        jnp.bfloat16
    )


def shards(
    embedding_activity,
    common_lookup_projector,
    content_projector,
    final_projector,
    lane_sharpness,
    sorted_place_per_element,
    element_per_sorted_place,
):
    n_dev = lax.axis_size("span")
    rows_here = embedding_activity.shape[0]
    capacity = 2 * rows_here // n_dev
    n_rounds = sorted_place_per_element.shape[0]
    per_peer = n_rounds * capacity
    buffer_rows = n_dev * per_peer
    head_cols = common_lookup_projector.shape[1]
    heads_here = head_cols // HEAD_DIM
    blocks_here = rows_here // BLOCK
    round_ids = jnp.arange(n_rounds, dtype=jnp.int32)[:, None]
    local_ids = jnp.broadcast_to(
        jnp.arange(rows_here, dtype=jnp.int32)[None, :], (n_rounds, rows_here)
    )

    target = sorted_place_per_element // rows_here
    send_rank = rank_within_group(target, local_ids)
    send_row = target * per_peer + round_ids * capacity + send_rank
    send_hot = one_hot_rows(send_row, buffer_rows)

    source = element_per_sorted_place // rows_here
    within = element_per_sorted_place % rows_here
    recv_rank = rank_within_group(source, within)
    recv_row = source * per_peer + round_ids * capacity + recv_rank
    recv_hot = one_hot_rows(recv_row, buffer_rows)

    full_projector = lax.all_gather(final_projector, "head", axis=0, tiled=True)
    outgoing = jnp.einsum(
        "rtq,tf->qf", send_hot, embedding_activity, preferred_element_type=jnp.float32
    ).astype(jnp.bfloat16)
    incoming = lax.all_to_all(outgoing, "span", split_axis=0, concat_axis=0, tiled=True)
    arrived = jnp.einsum(
        "rsq,qf->rsf", recv_hot, incoming, preferred_element_type=jnp.float32
    ).astype(jnp.bfloat16)
    prior_block = passed_along(arrived[:, rows_here - BLOCK :], "span", 1)
    with_prior = jnp.concatenate([prior_block, arrived], axis=1)
    full_rows = lax.all_gather(with_prior, "head", axis=2, tiled=True)
    normed = layer_norm(full_rows)
    joined = jnp.concatenate([common_lookup_projector, content_projector], axis=1)
    both = jnp.einsum(
        "rsf,fw->rsw", normed, joined, preferred_element_type=jnp.float32
    ).astype(jnp.bfloat16)
    span_rows = rows_here + BLOCK
    sorted_shared = both[:, :, :head_cols]
    sorted_values = both[:, :, head_cols:]
    spread = sorted_shared.reshape(n_rounds, span_rows, heads_here, HEAD_DIM).astype(jnp.float32)
    unitlength_address_lines = (
        spread * lax.rsqrt(jnp.sum(spread * spread, axis=-1, keepdims=True) + 1e-06)
    ).astype(jnp.bfloat16)
    unitlength_address_lines = unitlength_address_lines.reshape(n_rounds, span_rows, head_cols)
    keys_cur = unitlength_address_lines[:, BLOCK:].reshape(n_rounds, blocks_here, BLOCK, head_cols)
    key_rows = jnp.stack(
        [unitlength_address_lines[:, b * BLOCK : b * BLOCK + 2 * BLOCK] for b in range(blocks_here)],
        axis=1,
    ).reshape(n_rounds, blocks_here, 2 * BLOCK, heads_here, HEAD_DIM)
    content_projector_lines = jnp.stack(
        [sorted_values[:, b * BLOCK : b * BLOCK + 2 * BLOCK] for b in range(blocks_here)], axis=1
    ).reshape(n_rounds, blocks_here, 2 * BLOCK, heads_here, HEAD_DIM)
    queries = keys_cur.reshape(n_rounds, blocks_here, BLOCK, heads_here, HEAD_DIM)
    similarity_energies = jnp.einsum(
        "rbqhd,rbkhd->rbhqk", queries, key_rows, preferred_element_type=jnp.float32
    )
    similarity_energies = similarity_energies * lane_sharpness[None, None, :, None, None]
    allowed = jnp.arange(2 * BLOCK)[None, :] != jnp.arange(BLOCK)[:, None] + BLOCK
    exp_scores = jnp.where(allowed, jnp.exp(similarity_energies), 0.0)
    row_totals = jnp.sum(exp_scores, axis=-1)
    weights = (exp_scores / row_totals[..., None]).astype(jnp.bfloat16)
    results = jnp.einsum(
        "rbhqk,rbkhd->rbqhd", weights, content_projector_lines, preferred_element_type=jnp.float32
    )
    results = results.astype(jnp.bfloat16).reshape(n_rounds, rows_here, head_cols)
    slot_totals = jnp.transpose(row_totals, (0, 1, 3, 2)).reshape(n_rounds, rows_here, heads_here)
    totals_high = slot_totals.astype(jnp.bfloat16)
    totals_low = (slot_totals - totals_high.astype(jnp.float32)).astype(jnp.bfloat16)
    back_payload = jnp.concatenate([results, totals_high, totals_low], axis=2)

    back = jnp.einsum(
        "rsq,rsw->qw", recv_hot, back_payload, preferred_element_type=jnp.float32
    ).astype(jnp.bfloat16)
    home = lax.all_to_all(back, "span", split_axis=0, concat_axis=0, tiled=True)
    token_all = jnp.einsum("rtq,qw->rtw", send_hot, home, preferred_element_type=jnp.float32)
    token_rows = token_all[:, :, :head_cols]
    token_totals = (
        token_all[:, :, head_cols : head_cols + heads_here]
        + token_all[:, :, head_cols + heads_here : head_cols + 2 * heads_here]
    )
    round_share = token_totals / jnp.sum(token_totals, axis=0)
    token_spread = token_rows.reshape(n_rounds, rows_here, heads_here, HEAD_DIM)
    combined = jnp.sum(round_share[..., None] * token_spread, axis=0).astype(jnp.bfloat16)
    combined = combined.reshape(rows_here, head_cols)
    n_groups = lax.axis_size("head")
    mine = lax.all_to_all(combined, "head", split_axis=0, concat_axis=1, tiled=True)
    mine_rows = mine.shape[0]
    group_parts = jnp.einsum(
        "tgk,gkn->gtn",
        mine.reshape(mine_rows, n_groups, head_cols),
        full_projector.reshape(n_groups, head_cols, full_projector.shape[1]),
        preferred_element_type=jnp.float32,
    ).astype(jnp.bfloat16)
    return jnp.sum(group_parts.astype(jnp.float32), axis=0).astype(jnp.bfloat16)


def solution(mesh):
    placed = (
        P("span", "head"),
        P(None, "head"),
        P(None, "head"),
        P("head", None),
        P("head"),
        P(None, "span"),
        P(None, "span"),
    )
    return jax.shard_map(
        shards, mesh=mesh, in_specs=placed, out_specs=P(("span", "head"), None), check_vma=False
    )
```

```python
import jax
import jax.numpy as jnp
from jax import lax
from jax.sharding import PartitionSpec as P

HEAD_DIM = 128
BLOCK = 128


epsilon = 1e-05


def passed_along(block, axis, distance):
    devices = range(lax.axis_size(axis))
    route = [((i - distance) % len(devices), i) for i in devices]
    return lax.ppermute(block, axis, route)


def layer_norm(embedding_activity):
    content_embeddings = embedding_activity.astype(jnp.float32)
    row_mean = jnp.mean(content_embeddings, axis=-1, keepdims=True)
    centred = content_embeddings - row_mean
    row_var = jnp.mean(centred * centred, axis=-1, keepdims=True)
    return (centred * lax.rsqrt(row_var + epsilon)).astype(jnp.bfloat16)


def rank_within_group(group, order):
    same = group[:, :, None] == group[:, None, :]
    earlier = order[:, None, :] < order[:, :, None]
    return jnp.sum((same & earlier).astype(jnp.int32), axis=2)


def one_hot_rows(index, count):
    return (index[:, :, None] == jnp.arange(count, dtype=jnp.int32)[None, None, :]).astype(
        jnp.bfloat16
    )


def shards(
    embedding_activity,
    common_lookup_projector,
    content_projector,
    final_projector,
    lane_sharpness,
    sorted_place_per_element,
    element_per_sorted_place,
):
    n_dev = lax.axis_size("span")
    rows_here = embedding_activity.shape[0]
    capacity = 2 * rows_here // n_dev
    n_rounds = sorted_place_per_element.shape[0]
    per_peer = n_rounds * capacity
    buffer_rows = n_dev * per_peer
    head_cols = common_lookup_projector.shape[1]
    heads_here = head_cols // HEAD_DIM
    blocks_here = rows_here // BLOCK
    round_ids = jnp.arange(n_rounds, dtype=jnp.int32)[:, None]
    local_ids = jnp.broadcast_to(
        jnp.arange(rows_here, dtype=jnp.int32)[None, :], (n_rounds, rows_here)
    )

    target = sorted_place_per_element // rows_here
    send_rank = rank_within_group(target, local_ids)
    send_row = target * per_peer + round_ids * capacity + send_rank
    send_hot = one_hot_rows(send_row, buffer_rows)

    source = element_per_sorted_place // rows_here
    within = element_per_sorted_place % rows_here
    recv_rank = rank_within_group(source, within)
    recv_row = source * per_peer + round_ids * capacity + recv_rank
    recv_hot = one_hot_rows(recv_row, buffer_rows)

    outgoing = jnp.einsum(
        "rtq,tf->qf", send_hot, embedding_activity, preferred_element_type=jnp.float32
    ).astype(jnp.bfloat16)
    incoming = lax.all_to_all(outgoing, "span", split_axis=0, concat_axis=0, tiled=True)
    arrived = jnp.einsum(
        "rsq,qf->rsf", recv_hot, incoming, preferred_element_type=jnp.float32
    ).astype(jnp.bfloat16)
    prior_block = passed_along(arrived[:, rows_here - BLOCK :], "span", 1)
    with_prior = jnp.concatenate([prior_block, arrived], axis=1)
    n_groups = lax.axis_size("head")
    copies = jnp.broadcast_to(with_prior[None], (n_groups,) + with_prior.shape)
    gathered = lax.all_to_all(copies, "head", split_axis=0, concat_axis=0, tiled=True)
    full_rows = jnp.moveaxis(gathered, 0, 2).reshape(
        with_prior.shape[:2] + (n_groups * with_prior.shape[2],)
    )
    normed = layer_norm(full_rows)
    joined = jnp.concatenate([common_lookup_projector, content_projector], axis=1)
    both = jnp.einsum(
        "rsf,fw->rsw", normed, joined, preferred_element_type=jnp.float32
    ).astype(jnp.bfloat16)
    span_rows = rows_here + BLOCK
    sorted_shared = both[:, :, :head_cols]
    sorted_values = both[:, :, head_cols:]
    spread = sorted_shared.reshape(n_rounds, span_rows, heads_here, HEAD_DIM).astype(jnp.float32)
    unitlength_address_lines = (
        spread * lax.rsqrt(jnp.sum(spread * spread, axis=-1, keepdims=True) + 1e-06)
    ).astype(jnp.bfloat16)
    unitlength_address_lines = unitlength_address_lines.reshape(n_rounds, span_rows, head_cols)
    keys_cur = unitlength_address_lines[:, BLOCK:].reshape(n_rounds, blocks_here, BLOCK, head_cols)
    key_rows = jnp.stack(
        [unitlength_address_lines[:, b * BLOCK : b * BLOCK + 2 * BLOCK] for b in range(blocks_here)],
        axis=1,
    ).reshape(n_rounds, blocks_here, 2 * BLOCK, heads_here, HEAD_DIM)
    content_projector_lines = jnp.stack(
        [sorted_values[:, b * BLOCK : b * BLOCK + 2 * BLOCK] for b in range(blocks_here)], axis=1
    ).reshape(n_rounds, blocks_here, 2 * BLOCK, heads_here, HEAD_DIM)
    queries = keys_cur.reshape(n_rounds, blocks_here, BLOCK, heads_here, HEAD_DIM)
    similarity_energies = jnp.einsum(
        "rbqhd,rbkhd->rbhqk", queries, key_rows, preferred_element_type=jnp.float32
    )
    similarity_energies = similarity_energies * lane_sharpness[None, None, :, None, None]
    allowed = jnp.arange(2 * BLOCK)[None, :] != jnp.arange(BLOCK)[:, None] + BLOCK
    exp_scores = jnp.where(allowed, jnp.exp(similarity_energies), 0.0)
    row_totals = jnp.sum(exp_scores, axis=-1)
    weights = (exp_scores / row_totals[..., None]).astype(jnp.bfloat16)
    results = jnp.einsum(
        "rbhqk,rbkhd->rbqhd", weights, content_projector_lines, preferred_element_type=jnp.float32
    )
    results = results.astype(jnp.bfloat16).reshape(n_rounds, rows_here, head_cols)
    slot_totals = jnp.transpose(row_totals, (0, 1, 3, 2)).reshape(n_rounds, rows_here, heads_here)
    totals_high = slot_totals.astype(jnp.bfloat16)
    totals_low = (slot_totals - totals_high.astype(jnp.float32)).astype(jnp.bfloat16)
    back_payload = jnp.concatenate([results, totals_high, totals_low], axis=2)

    back = jnp.einsum(
        "rsq,rsw->qw", recv_hot, back_payload, preferred_element_type=jnp.float32
    ).astype(jnp.bfloat16)
    home = lax.all_to_all(back, "span", split_axis=0, concat_axis=0, tiled=True)
    token_all = jnp.einsum("rtq,qw->rtw", send_hot, home, preferred_element_type=jnp.float32)
    token_rows = token_all[:, :, :head_cols]
    token_totals = (
        token_all[:, :, head_cols : head_cols + heads_here]
        + token_all[:, :, head_cols + heads_here : head_cols + 2 * heads_here]
    )
    round_share = token_totals / jnp.sum(token_totals, axis=0)
    token_spread = token_rows.reshape(n_rounds, rows_here, heads_here, HEAD_DIM)
    combined = jnp.sum(round_share[..., None] * token_spread, axis=0).astype(jnp.bfloat16)
    combined = combined.reshape(rows_here, head_cols)
    group_part = jnp.dot(
        combined, final_projector, preferred_element_type=jnp.float32
    ).astype(jnp.bfloat16)
    group_parts = lax.all_to_all(
        group_part.reshape(n_groups, rows_here // n_groups, group_part.shape[1]),
        "head",
        split_axis=0,
        concat_axis=0,
        tiled=True,
    )
    return jnp.sum(group_parts.astype(jnp.float32), axis=0).astype(jnp.bfloat16)


def solution(mesh):
    placed = (
        P("span", "head"),
        P(None, "head"),
        P(None, "head"),
        P("head", None),
        P("head"),
        P(None, "span"),
        P(None, "span"),
    )
    return jax.shard_map(
        shards, mesh=mesh, in_specs=placed, out_specs=P(("span", "head"), None), check_vma=False
    )
```

```python
import jax
import jax.numpy as jnp
from jax import lax
from jax.sharding import PartitionSpec as P

HEAD_DIM = 128
BLOCK = 128


epsilon = 1e-05


def passed_along(block, axis, distance):
    devices = range(lax.axis_size(axis))
    route = [((i - distance) % len(devices), i) for i in devices]
    return lax.ppermute(block, axis, route)


def layer_norm(embedding_activity):
    content_embeddings = embedding_activity.astype(jnp.float32)
    row_mean = jnp.mean(content_embeddings, axis=-1, keepdims=True)
    centred = content_embeddings - row_mean
    row_var = jnp.mean(centred * centred, axis=-1, keepdims=True)
    return (centred * lax.rsqrt(row_var + epsilon)).astype(jnp.bfloat16)


def rank_within_group(group, order):
    same = group[:, :, None] == group[:, None, :]
    earlier = order[:, None, :] < order[:, :, None]
    return jnp.sum((same & earlier).astype(jnp.int32), axis=2)


def one_hot_rows(index, count):
    return (index[:, :, None] == jnp.arange(count, dtype=jnp.int32)[None, None, :]).astype(
        jnp.bfloat16
    )


def shards(
    embedding_activity,
    common_lookup_projector,
    content_projector,
    final_projector,
    lane_sharpness,
    sorted_place_per_element,
    element_per_sorted_place,
):
    n_dev = lax.axis_size("span")
    rows_here = embedding_activity.shape[0]
    capacity = 2 * rows_here // n_dev
    n_rounds = sorted_place_per_element.shape[0]
    per_peer = n_rounds * capacity
    buffer_rows = n_dev * per_peer
    head_cols = common_lookup_projector.shape[1]
    heads_here = head_cols // HEAD_DIM
    blocks_here = rows_here // BLOCK
    round_ids = jnp.arange(n_rounds, dtype=jnp.int32)[:, None]
    local_ids = jnp.broadcast_to(
        jnp.arange(rows_here, dtype=jnp.int32)[None, :], (n_rounds, rows_here)
    )

    target = sorted_place_per_element // rows_here
    send_rank = rank_within_group(target, local_ids)
    send_row = target * per_peer + round_ids * capacity + send_rank
    send_hot = one_hot_rows(send_row, buffer_rows)

    source = element_per_sorted_place // rows_here
    within = element_per_sorted_place % rows_here
    recv_rank = rank_within_group(source, within)
    recv_row = source * per_peer + round_ids * capacity + recv_rank
    recv_hot = one_hot_rows(recv_row, buffer_rows)

    outgoing = jnp.einsum(
        "rtq,tf->qf", send_hot, embedding_activity, preferred_element_type=jnp.float32
    ).astype(jnp.bfloat16)
    incoming = lax.all_to_all(outgoing, "span", split_axis=0, concat_axis=0, tiled=True)
    arrived = jnp.einsum(
        "rsq,qf->rsf", recv_hot, incoming, preferred_element_type=jnp.float32
    ).astype(jnp.bfloat16)
    prior_block = passed_along(arrived[:, rows_here - BLOCK :], "span", 1)
    n_groups = lax.axis_size("head")
    joined = jnp.concatenate([common_lookup_projector, content_projector], axis=1)

    def gather_features(rows):
        copies = jnp.broadcast_to(rows[None], (n_groups,) + rows.shape)
        return lax.all_to_all(copies, "head", split_axis=0, concat_axis=0, tiled=True)

    def keys_and_values(gathered):
        rows_shape = gathered.shape[1:3]
        full_rows = jnp.moveaxis(gathered, 0, 2).reshape(rows_shape + (-1,))
        normed = layer_norm(full_rows)
        both = jnp.einsum(
            "rsf,fw->rsw", normed, joined, preferred_element_type=jnp.float32
        ).astype(jnp.bfloat16)
        spread = both[:, :, :head_cols].reshape(rows_shape + (heads_here, HEAD_DIM))
        spread = spread.astype(jnp.float32)
        unit = (
            spread * lax.rsqrt(jnp.sum(spread * spread, axis=-1, keepdims=True) + 1e-06)
        ).astype(jnp.bfloat16)
        return unit.reshape(rows_shape + (head_cols,)), both[:, :, head_cols:]

    gathered_here = gather_features(arrived)
    prior_block, gathered_here = lax.optimization_barrier((prior_block, gathered_here))
    gathered_prior = gather_features(prior_block)
    keys_here, values_here = keys_and_values(gathered_here)
    keys_prior, values_prior = keys_and_values(gathered_prior)
    unitlength_address_lines = jnp.concatenate([keys_prior, keys_here], axis=1)
    sorted_values = jnp.concatenate([values_prior, values_here], axis=1)
    keys_cur = unitlength_address_lines[:, BLOCK:].reshape(n_rounds, blocks_here, BLOCK, head_cols)
    key_rows = jnp.stack(
        [unitlength_address_lines[:, b * BLOCK : b * BLOCK + 2 * BLOCK] for b in range(blocks_here)],
        axis=1,
    ).reshape(n_rounds, blocks_here, 2 * BLOCK, heads_here, HEAD_DIM)
    content_projector_lines = jnp.stack(
        [sorted_values[:, b * BLOCK : b * BLOCK + 2 * BLOCK] for b in range(blocks_here)], axis=1
    ).reshape(n_rounds, blocks_here, 2 * BLOCK, heads_here, HEAD_DIM)
    queries = keys_cur.reshape(n_rounds, blocks_here, BLOCK, heads_here, HEAD_DIM)
    similarity_energies = jnp.einsum(
        "rbqhd,rbkhd->rbhqk", queries, key_rows, preferred_element_type=jnp.float32
    )
    similarity_energies = similarity_energies * lane_sharpness[None, None, :, None, None]
    allowed = jnp.arange(2 * BLOCK)[None, :] != jnp.arange(BLOCK)[:, None] + BLOCK
    exp_scores = jnp.where(allowed, jnp.exp(similarity_energies), 0.0)
    row_totals = jnp.sum(exp_scores, axis=-1)
    weights = (exp_scores / row_totals[..., None]).astype(jnp.bfloat16)
    results = jnp.einsum(
        "rbhqk,rbkhd->rbqhd", weights, content_projector_lines, preferred_element_type=jnp.float32
    )
    results = results.astype(jnp.bfloat16).reshape(n_rounds, rows_here, head_cols)
    slot_totals = jnp.transpose(row_totals, (0, 1, 3, 2)).reshape(n_rounds, rows_here, heads_here)
    totals_high = slot_totals.astype(jnp.bfloat16)
    totals_low = (slot_totals - totals_high.astype(jnp.float32)).astype(jnp.bfloat16)
    back_payload = jnp.concatenate([results, totals_high, totals_low], axis=2)

    back = jnp.einsum(
        "rsq,rsw->qw", recv_hot, back_payload, preferred_element_type=jnp.float32
    ).astype(jnp.bfloat16)
    home = lax.all_to_all(back, "span", split_axis=0, concat_axis=0, tiled=True)
    token_all = jnp.einsum("rtq,qw->rtw", send_hot, home, preferred_element_type=jnp.float32)
    token_rows = token_all[:, :, :head_cols]
    token_totals = (
        token_all[:, :, head_cols : head_cols + heads_here]
        + token_all[:, :, head_cols + heads_here : head_cols + 2 * heads_here]
    )
    round_share = token_totals / jnp.sum(token_totals, axis=0)
    token_spread = token_rows.reshape(n_rounds, rows_here, heads_here, HEAD_DIM)
    combined = jnp.sum(round_share[..., None] * token_spread, axis=0).astype(jnp.bfloat16)
    combined = combined.reshape(rows_here, head_cols)
    group_part = jnp.dot(
        combined, final_projector, preferred_element_type=jnp.float32
    ).astype(jnp.bfloat16)
    group_parts = lax.all_to_all(
        group_part.reshape(n_groups, rows_here // n_groups, group_part.shape[1]),
        "head",
        split_axis=0,
        concat_axis=0,
        tiled=True,
    )
    return jnp.sum(group_parts.astype(jnp.float32), axis=0).astype(jnp.bfloat16)


def solution(mesh):
    placed = (
        P("span", "head"),
        P(None, "head"),
        P(None, "head"),
        P("head", None),
        P("head"),
        P(None, "span"),
        P(None, "span"),
    )
    return jax.shard_map(
        shards, mesh=mesh, in_specs=placed, out_specs=P(("span", "head"), None), check_vma=False
    )
```

```python
import jax
import jax.numpy as jnp
from jax import lax
from jax.sharding import PartitionSpec as P

HEAD_DIM = 128
BLOCK = 128


epsilon = 1e-05


def passed_along(block, axis, distance):
    devices = range(lax.axis_size(axis))
    route = [((i - distance) % len(devices), i) for i in devices]
    return lax.ppermute(block, axis, route)


def layer_norm(embedding_activity):
    content_embeddings = embedding_activity.astype(jnp.float32)
    row_mean = jnp.mean(content_embeddings, axis=-1, keepdims=True)
    centred = content_embeddings - row_mean
    row_var = jnp.mean(centred * centred, axis=-1, keepdims=True)
    return (centred * lax.rsqrt(row_var + epsilon)).astype(jnp.bfloat16)


def rank_within_group(group, order):
    same = group[:, :, None] == group[:, None, :]
    earlier = order[:, None, :] < order[:, :, None]
    return jnp.sum((same & earlier).astype(jnp.int32), axis=2)


def one_hot_rows(index, count):
    return (index[:, :, None] == jnp.arange(count, dtype=jnp.int32)[None, None, :]).astype(
        jnp.bfloat16
    )


def shards(
    embedding_activity,
    common_lookup_projector,
    content_projector,
    final_projector,
    lane_sharpness,
    sorted_place_per_element,
    element_per_sorted_place,
):
    n_dev = lax.axis_size("span")
    rows_here = embedding_activity.shape[0]
    capacity = 2 * rows_here // n_dev
    n_rounds = sorted_place_per_element.shape[0]
    per_peer = n_rounds * capacity
    buffer_rows = n_dev * per_peer
    head_cols = common_lookup_projector.shape[1]
    heads_here = head_cols // HEAD_DIM
    blocks_here = rows_here // BLOCK
    round_ids = jnp.arange(n_rounds, dtype=jnp.int32)[:, None]
    local_ids = jnp.broadcast_to(
        jnp.arange(rows_here, dtype=jnp.int32)[None, :], (n_rounds, rows_here)
    )

    target = sorted_place_per_element // rows_here
    send_rank = rank_within_group(target, local_ids)
    send_row = target * per_peer + round_ids * capacity + send_rank
    send_hot = one_hot_rows(send_row, buffer_rows)

    source = element_per_sorted_place // rows_here
    within = element_per_sorted_place % rows_here
    recv_rank = rank_within_group(source, within)
    recv_row = source * per_peer + round_ids * capacity + recv_rank
    recv_hot = one_hot_rows(recv_row, buffer_rows)

    outgoing = jnp.einsum(
        "rtq,tf->qf", send_hot, embedding_activity, preferred_element_type=jnp.float32
    ).astype(jnp.bfloat16)
    incoming = lax.all_to_all(outgoing, "span", split_axis=0, concat_axis=0, tiled=True)
    arrived = jnp.einsum(
        "rsq,qf->rsf", recv_hot, incoming, preferred_element_type=jnp.float32
    ).astype(jnp.bfloat16)
    prior_block = passed_along(arrived[:, rows_here - BLOCK :], "span", 1)
    n_groups = lax.axis_size("head")
    joined = jnp.concatenate([common_lookup_projector, content_projector], axis=1)

    def gather_features(rows):
        copies = jnp.broadcast_to(rows[None], (n_groups,) + rows.shape)
        return lax.all_to_all(copies, "head", split_axis=0, concat_axis=0, tiled=True)

    def keys_and_values(gathered):
        rows_shape = gathered.shape[1:3]
        full_rows = jnp.moveaxis(gathered, 0, 2).reshape(rows_shape + (-1,))
        normed = layer_norm(full_rows)
        both = jnp.einsum(
            "rsf,fw->rsw", normed, joined, preferred_element_type=jnp.float32
        ).astype(jnp.bfloat16)
        spread = both[:, :, :head_cols].reshape(rows_shape + (heads_here, HEAD_DIM))
        spread = spread.astype(jnp.float32)
        unit = (
            spread * lax.rsqrt(jnp.sum(spread * spread, axis=-1, keepdims=True) + 1e-06)
        ).astype(jnp.bfloat16)
        return unit.reshape(rows_shape + (head_cols,)), both[:, :, head_cols:]

    gathered_here = gather_features(arrived)
    prior_block, gathered_here = lax.optimization_barrier((prior_block, gathered_here))
    gathered_prior = gather_features(prior_block)
    keys_here, values_here = keys_and_values(gathered_here)
    keys_prior, values_prior = keys_and_values(gathered_prior)
    unitlength_address_lines = jnp.concatenate([keys_prior, keys_here], axis=1)
    sorted_values = jnp.concatenate([values_prior, values_here], axis=1)
    keys_cur = unitlength_address_lines[:, BLOCK:].reshape(n_rounds, blocks_here, BLOCK, head_cols)
    key_rows = jnp.stack(
        [unitlength_address_lines[:, b * BLOCK : b * BLOCK + 2 * BLOCK] for b in range(blocks_here)],
        axis=1,
    ).reshape(n_rounds, blocks_here, 2 * BLOCK, heads_here, HEAD_DIM)
    content_projector_lines = jnp.stack(
        [sorted_values[:, b * BLOCK : b * BLOCK + 2 * BLOCK] for b in range(blocks_here)], axis=1
    ).reshape(n_rounds, blocks_here, 2 * BLOCK, heads_here, HEAD_DIM)
    queries = keys_cur.reshape(n_rounds, blocks_here, BLOCK, heads_here, HEAD_DIM)
    similarity_energies = jnp.einsum(
        "rbqhd,rbkhd->rbhqk", queries, key_rows, preferred_element_type=jnp.float32
    )
    similarity_energies = similarity_energies * lane_sharpness[None, None, :, None, None]
    allowed = jnp.arange(2 * BLOCK)[None, :] != jnp.arange(BLOCK)[:, None] + BLOCK
    exp_scores = jnp.where(allowed, jnp.exp(similarity_energies), 0.0)
    row_totals = jnp.sum(exp_scores, axis=-1)
    weights = (exp_scores / row_totals[..., None]).astype(jnp.bfloat16)
    results = jnp.einsum(
        "rbhqk,rbkhd->rbqhd", weights, content_projector_lines, preferred_element_type=jnp.float32
    )
    results = results.astype(jnp.bfloat16).reshape(n_rounds, rows_here, head_cols)
    slot_totals = jnp.transpose(row_totals, (0, 1, 3, 2)).reshape(n_rounds, rows_here, heads_here)
    totals_high = slot_totals.astype(jnp.bfloat16)
    totals_low = (slot_totals - totals_high.astype(jnp.float32)).astype(jnp.bfloat16)
    back_payload = jnp.concatenate([results, totals_high, totals_low], axis=2)

    back = jnp.einsum(
        "rsq,rsw->qw", recv_hot, back_payload, preferred_element_type=jnp.float32
    ).astype(jnp.bfloat16)
    back_width = back.shape[1]
    back = lax.optimization_barrier(back).reshape(n_dev, per_peer * back_width)
    home = lax.all_to_all(back, "span", split_axis=0, concat_axis=0, tiled=True)
    home = lax.optimization_barrier(home.reshape(buffer_rows, back_width))
    token_all = jnp.einsum("rtq,qw->rtw", send_hot, home, preferred_element_type=jnp.float32)
    token_rows = token_all[:, :, :head_cols]
    token_totals = (
        token_all[:, :, head_cols : head_cols + heads_here]
        + token_all[:, :, head_cols + heads_here : head_cols + 2 * heads_here]
    )
    round_share = token_totals / jnp.sum(token_totals, axis=0)
    token_spread = token_rows.reshape(n_rounds, rows_here, heads_here, HEAD_DIM)
    combined = jnp.sum(round_share[..., None] * token_spread, axis=0).astype(jnp.bfloat16)
    combined = combined.reshape(rows_here, head_cols)
    group_part = jnp.dot(
        combined, final_projector, preferred_element_type=jnp.float32
    ).astype(jnp.bfloat16)
    group_parts = lax.all_to_all(
        group_part.reshape(n_groups, rows_here // n_groups, group_part.shape[1]),
        "head",
        split_axis=0,
        concat_axis=0,
        tiled=True,
    )
    return jnp.sum(group_parts.astype(jnp.float32), axis=0).astype(jnp.bfloat16)


def solution(mesh):
    placed = (
        P("span", "head"),
        P(None, "head"),
        P(None, "head"),
        P("head", None),
        P("head"),
        P(None, "span"),
        P(None, "span"),
    )
    return jax.shard_map(
        shards, mesh=mesh, in_specs=placed, out_specs=P(("span", "head"), None), check_vma=False
    )
```

```python
import jax
import jax.numpy as jnp
from jax import lax
from jax.sharding import PartitionSpec as P

HEAD_DIM = 128
BLOCK = 128


epsilon = 1e-05


def passed_along(block, axis, distance):
    devices = range(lax.axis_size(axis))
    route = [((i - distance) % len(devices), i) for i in devices]
    return lax.ppermute(block, axis, route)


def layer_norm(embedding_activity):
    content_embeddings = embedding_activity.astype(jnp.float32)
    row_mean = jnp.mean(content_embeddings, axis=-1, keepdims=True)
    centred = content_embeddings - row_mean
    row_var = jnp.mean(centred * centred, axis=-1, keepdims=True)
    return (centred * lax.rsqrt(row_var + epsilon)).astype(jnp.bfloat16)


def rank_within_group(group, order):
    same = group[:, :, None] == group[:, None, :]
    earlier = order[:, None, :] < order[:, :, None]
    return jnp.sum((same & earlier).astype(jnp.int32), axis=2)


def one_hot_rows(index, count):
    return (index[:, :, None] == jnp.arange(count, dtype=jnp.int32)[None, None, :]).astype(
        jnp.bfloat16
    )


def shards(
    embedding_activity,
    common_lookup_projector,
    content_projector,
    final_projector,
    lane_sharpness,
    sorted_place_per_element,
    element_per_sorted_place,
):
    n_dev = lax.axis_size("span")
    rows_here = embedding_activity.shape[0]
    capacity = 2 * rows_here // n_dev
    n_rounds = sorted_place_per_element.shape[0]
    per_peer = n_rounds * capacity
    buffer_rows = n_dev * per_peer
    head_cols = common_lookup_projector.shape[1]
    heads_here = head_cols // HEAD_DIM
    blocks_here = rows_here // BLOCK
    round_ids = jnp.arange(n_rounds, dtype=jnp.int32)[:, None]
    local_ids = jnp.broadcast_to(
        jnp.arange(rows_here, dtype=jnp.int32)[None, :], (n_rounds, rows_here)
    )

    target = sorted_place_per_element // rows_here
    send_rank = rank_within_group(target, local_ids)
    send_row = target * per_peer + round_ids * capacity + send_rank
    send_hot = one_hot_rows(send_row, buffer_rows)

    source = element_per_sorted_place // rows_here
    within = element_per_sorted_place % rows_here
    recv_rank = rank_within_group(source, within)
    recv_row = source * per_peer + round_ids * capacity + recv_rank
    recv_hot = one_hot_rows(recv_row, buffer_rows)

    outgoing = jnp.einsum(
        "rtq,tf->qf", send_hot, embedding_activity, preferred_element_type=jnp.float32
    ).astype(jnp.bfloat16)
    incoming = lax.all_to_all(outgoing, "span", split_axis=0, concat_axis=0, tiled=True)
    arrived = jnp.einsum(
        "rsq,qf->rsf", recv_hot, incoming, preferred_element_type=jnp.float32
    ).astype(jnp.bfloat16)
    n_groups = lax.axis_size("head")
    joined = jnp.concatenate([common_lookup_projector, content_projector], axis=1)
    copies = jnp.broadcast_to(arrived[None], (n_groups,) + arrived.shape)
    gathered = lax.all_to_all(copies, "head", split_axis=0, concat_axis=0, tiled=True)
    full_rows = jnp.moveaxis(gathered, 0, 2).reshape(arrived.shape[:2] + (-1,))
    normed = layer_norm(full_rows)
    both = jnp.einsum(
        "rsf,fw->rsw", normed, joined, preferred_element_type=jnp.float32
    ).astype(jnp.bfloat16)
    spread = both[:, :, :head_cols].reshape(n_rounds, rows_here, heads_here, HEAD_DIM)
    spread = spread.astype(jnp.float32)
    keys_here = (
        spread * lax.rsqrt(jnp.sum(spread * spread, axis=-1, keepdims=True) + 1e-06)
    ).astype(jnp.bfloat16).reshape(n_rounds, rows_here, head_cols)
    values_here = both[:, :, head_cols:]
    last_block = jnp.concatenate(
        [keys_here[:, rows_here - BLOCK :], values_here[:, rows_here - BLOCK :]], axis=2
    )
    prior_block = passed_along(last_block, "span", 1)
    unitlength_address_lines = jnp.concatenate([prior_block[:, :, :head_cols], keys_here], axis=1)
    sorted_values = jnp.concatenate([prior_block[:, :, head_cols:], values_here], axis=1)
    keys_cur = unitlength_address_lines[:, BLOCK:].reshape(n_rounds, blocks_here, BLOCK, head_cols)
    key_rows = jnp.stack(
        [unitlength_address_lines[:, b * BLOCK : b * BLOCK + 2 * BLOCK] for b in range(blocks_here)],
        axis=1,
    ).reshape(n_rounds, blocks_here, 2 * BLOCK, heads_here, HEAD_DIM)
    content_projector_lines = jnp.stack(
        [sorted_values[:, b * BLOCK : b * BLOCK + 2 * BLOCK] for b in range(blocks_here)], axis=1
    ).reshape(n_rounds, blocks_here, 2 * BLOCK, heads_here, HEAD_DIM)
    queries = keys_cur.reshape(n_rounds, blocks_here, BLOCK, heads_here, HEAD_DIM)
    similarity_energies = jnp.einsum(
        "rbqhd,rbkhd->rbhqk", queries, key_rows, preferred_element_type=jnp.float32
    )
    similarity_energies = similarity_energies * lane_sharpness[None, None, :, None, None]
    allowed = jnp.arange(2 * BLOCK)[None, :] != jnp.arange(BLOCK)[:, None] + BLOCK
    exp_scores = jnp.where(allowed, jnp.exp(similarity_energies), 0.0)
    row_totals = jnp.sum(exp_scores, axis=-1)
    weights = (exp_scores / row_totals[..., None]).astype(jnp.bfloat16)
    results = jnp.einsum(
        "rbhqk,rbkhd->rbqhd", weights, content_projector_lines, preferred_element_type=jnp.float32
    )
    results = results.astype(jnp.bfloat16).reshape(n_rounds, rows_here, head_cols)
    slot_totals = jnp.transpose(row_totals, (0, 1, 3, 2)).reshape(n_rounds, rows_here, heads_here)
    totals_high = slot_totals.astype(jnp.bfloat16)
    totals_low = (slot_totals - totals_high.astype(jnp.float32)).astype(jnp.bfloat16)
    back_payload = jnp.concatenate([results, totals_high, totals_low], axis=2)

    back = jnp.einsum(
        "rsq,rsw->qw", recv_hot, back_payload, preferred_element_type=jnp.float32
    ).astype(jnp.bfloat16)
    home = lax.all_to_all(back, "span", split_axis=0, concat_axis=0, tiled=True)
    token_all = jnp.einsum("rtq,qw->rtw", send_hot, home, preferred_element_type=jnp.float32)
    token_rows = token_all[:, :, :head_cols]
    token_totals = (
        token_all[:, :, head_cols : head_cols + heads_here]
        + token_all[:, :, head_cols + heads_here : head_cols + 2 * heads_here]
    )
    round_share = token_totals / jnp.sum(token_totals, axis=0)
    token_spread = token_rows.reshape(n_rounds, rows_here, heads_here, HEAD_DIM)
    combined = jnp.sum(round_share[..., None] * token_spread, axis=0).astype(jnp.bfloat16)
    combined = combined.reshape(rows_here, head_cols)
    group_part = jnp.dot(
        combined, final_projector, preferred_element_type=jnp.float32
    ).astype(jnp.bfloat16)
    group_parts = lax.all_to_all(
        group_part.reshape(n_groups, rows_here // n_groups, group_part.shape[1]),
        "head",
        split_axis=0,
        concat_axis=0,
        tiled=True,
    )
    return jnp.sum(group_parts.astype(jnp.float32), axis=0).astype(jnp.bfloat16)


def solution(mesh):
    placed = (
        P("span", "head"),
        P(None, "head"),
        P(None, "head"),
        P("head", None),
        P("head"),
        P(None, "span"),
        P(None, "span"),
    )
    return jax.shard_map(
        shards, mesh=mesh, in_specs=placed, out_specs=P(("span", "head"), None), check_vma=False
    )
```

```python
import jax
import jax.numpy as jnp
from jax import lax
from jax.sharding import PartitionSpec as P

HEAD_DIM = 128
BLOCK = 128


epsilon = 1e-05


def passed_along(block, axis, distance):
    devices = range(lax.axis_size(axis))
    route = [((i - distance) % len(devices), i) for i in devices]
    return lax.ppermute(block, axis, route)


def layer_norm(embedding_activity):
    content_embeddings = embedding_activity.astype(jnp.float32)
    row_mean = jnp.mean(content_embeddings, axis=-1, keepdims=True)
    centred = content_embeddings - row_mean
    row_var = jnp.mean(centred * centred, axis=-1, keepdims=True)
    return (centred * lax.rsqrt(row_var + epsilon)).astype(jnp.bfloat16)


def rank_within_group(group, order):
    same = group[:, :, None] == group[:, None, :]
    earlier = order[:, None, :] < order[:, :, None]
    return jnp.sum((same & earlier).astype(jnp.int32), axis=2)


def one_hot_rows(index, count):
    return (index[:, :, None] == jnp.arange(count, dtype=jnp.int32)[None, None, :]).astype(
        jnp.bfloat16
    )


def shards(
    embedding_activity,
    common_lookup_projector,
    content_projector,
    final_projector,
    lane_sharpness,
    sorted_place_per_element,
    element_per_sorted_place,
):
    n_dev = lax.axis_size("span")
    rows_here = embedding_activity.shape[0]
    capacity = 2 * rows_here // n_dev
    n_rounds = sorted_place_per_element.shape[0]
    per_peer = n_rounds * capacity
    buffer_rows = n_dev * per_peer
    head_cols = common_lookup_projector.shape[1]
    heads_here = head_cols // HEAD_DIM
    blocks_here = rows_here // BLOCK
    round_ids = jnp.arange(n_rounds, dtype=jnp.int32)[:, None]
    local_ids = jnp.broadcast_to(
        jnp.arange(rows_here, dtype=jnp.int32)[None, :], (n_rounds, rows_here)
    )

    target = sorted_place_per_element // rows_here
    send_rank = rank_within_group(target, local_ids)
    send_row = target * per_peer + round_ids * capacity + send_rank
    send_hot = one_hot_rows(send_row, buffer_rows)

    source = element_per_sorted_place // rows_here
    within = element_per_sorted_place % rows_here
    recv_rank = rank_within_group(source, within)
    recv_row = source * per_peer + round_ids * capacity + recv_rank
    recv_hot = one_hot_rows(recv_row, buffer_rows)

    outgoing = jnp.einsum(
        "rtq,tf->qf", send_hot, embedding_activity, preferred_element_type=jnp.float32
    ).astype(jnp.bfloat16)
    incoming = lax.all_to_all(outgoing, "span", split_axis=0, concat_axis=0, tiled=True)
    arrived = jnp.einsum(
        "rsq,qf->rsf", recv_hot, incoming, preferred_element_type=jnp.float32
    ).astype(jnp.bfloat16)
    n_groups = lax.axis_size("head")
    joined = jnp.concatenate([common_lookup_projector, content_projector], axis=1)
    copies = jnp.broadcast_to(arrived[None], (n_groups,) + arrived.shape)
    gathered = lax.all_to_all(copies, "head", split_axis=0, concat_axis=0, tiled=True)
    last_slice = arrived[:, rows_here - BLOCK :]
    received = []
    for shift in range(n_groups):
        route = [
            (s * n_groups + g, ((s + 1) % n_dev) * n_groups + (g + shift) % n_groups)
            for s in range(n_dev)
            for g in range(n_groups)
        ]
        received.append(lax.ppermute(last_slice, ("span", "head"), route))
    received, gathered = lax.optimization_barrier((received, gathered))
    group_here = lax.axis_index("head")
    slice_order = (group_here - jnp.arange(n_groups, dtype=jnp.int32)) % n_groups
    prior_slices = jnp.take(jnp.stack(received), slice_order, axis=0)
    all_slices = jnp.concatenate([prior_slices, gathered], axis=2)
    span_rows = rows_here + BLOCK
    full_rows = jnp.moveaxis(all_slices, 0, 2).reshape(n_rounds, span_rows, -1)
    normed = layer_norm(full_rows)
    both = jnp.einsum(
        "rsf,fw->rsw", normed, joined, preferred_element_type=jnp.float32
    ).astype(jnp.bfloat16)
    spread = both[:, :, :head_cols].reshape(n_rounds, span_rows, heads_here, HEAD_DIM)
    spread = spread.astype(jnp.float32)
    unitlength_address_lines = (
        spread * lax.rsqrt(jnp.sum(spread * spread, axis=-1, keepdims=True) + 1e-06)
    ).astype(jnp.bfloat16).reshape(n_rounds, span_rows, head_cols)
    sorted_values = both[:, :, head_cols:]
    keys_cur = unitlength_address_lines[:, BLOCK:].reshape(n_rounds, blocks_here, BLOCK, head_cols)
    key_rows = jnp.stack(
        [unitlength_address_lines[:, b * BLOCK : b * BLOCK + 2 * BLOCK] for b in range(blocks_here)],
        axis=1,
    ).reshape(n_rounds, blocks_here, 2 * BLOCK, heads_here, HEAD_DIM)
    content_projector_lines = jnp.stack(
        [sorted_values[:, b * BLOCK : b * BLOCK + 2 * BLOCK] for b in range(blocks_here)], axis=1
    ).reshape(n_rounds, blocks_here, 2 * BLOCK, heads_here, HEAD_DIM)
    queries = keys_cur.reshape(n_rounds, blocks_here, BLOCK, heads_here, HEAD_DIM)
    similarity_energies = jnp.einsum(
        "rbqhd,rbkhd->rbhqk", queries, key_rows, preferred_element_type=jnp.float32
    )
    similarity_energies = similarity_energies * lane_sharpness[None, None, :, None, None]
    allowed = jnp.arange(2 * BLOCK)[None, :] != jnp.arange(BLOCK)[:, None] + BLOCK
    exp_scores = jnp.where(allowed, jnp.exp(similarity_energies), 0.0)
    row_totals = jnp.sum(exp_scores, axis=-1)
    weights = (exp_scores / row_totals[..., None]).astype(jnp.bfloat16)
    results = jnp.einsum(
        "rbhqk,rbkhd->rbqhd", weights, content_projector_lines, preferred_element_type=jnp.float32
    )
    results = results.astype(jnp.bfloat16).reshape(n_rounds, rows_here, head_cols)
    slot_totals = jnp.transpose(row_totals, (0, 1, 3, 2)).reshape(n_rounds, rows_here, heads_here)
    totals_high = slot_totals.astype(jnp.bfloat16)
    totals_low = (slot_totals - totals_high.astype(jnp.float32)).astype(jnp.bfloat16)
    back_payload = jnp.concatenate([results, totals_high, totals_low], axis=2)

    back = jnp.einsum(
        "rsq,rsw->qw", recv_hot, back_payload, preferred_element_type=jnp.float32
    ).astype(jnp.bfloat16)
    home = lax.all_to_all(back, "span", split_axis=0, concat_axis=0, tiled=True)
    token_all = jnp.einsum("rtq,qw->rtw", send_hot, home, preferred_element_type=jnp.float32)
    token_rows = token_all[:, :, :head_cols]
    token_totals = (
        token_all[:, :, head_cols : head_cols + heads_here]
        + token_all[:, :, head_cols + heads_here : head_cols + 2 * heads_here]
    )
    round_share = token_totals / jnp.sum(token_totals, axis=0)
    token_spread = token_rows.reshape(n_rounds, rows_here, heads_here, HEAD_DIM)
    combined = jnp.sum(round_share[..., None] * token_spread, axis=0).astype(jnp.bfloat16)
    combined = combined.reshape(rows_here, head_cols)
    group_part = jnp.dot(
        combined, final_projector, preferred_element_type=jnp.float32
    ).astype(jnp.bfloat16)
    group_parts = lax.all_to_all(
        group_part.reshape(n_groups, rows_here // n_groups, group_part.shape[1]),
        "head",
        split_axis=0,
        concat_axis=0,
        tiled=True,
    )
    return jnp.sum(group_parts.astype(jnp.float32), axis=0).astype(jnp.bfloat16)


def solution(mesh):
    placed = (
        P("span", "head"),
        P(None, "head"),
        P(None, "head"),
        P("head", None),
        P("head"),
        P(None, "span"),
        P(None, "span"),
    )
    return jax.shard_map(
        shards, mesh=mesh, in_specs=placed, out_specs=P(("span", "head"), None), check_vma=False
    )
```

```python
import jax
import jax.numpy as jnp
from jax import lax
from jax.experimental import pallas as pl
from jax.experimental.pallas import tpu as pltpu
from jax.sharding import PartitionSpec as P

HEAD_DIM = 128
BLOCK = 128


epsilon = 1e-05


def passed_along(block, axis, distance):
    devices = range(lax.axis_size(axis))
    route = [((i - distance) % len(devices), i) for i in devices]
    return lax.ppermute(block, axis, route)


def layer_norm(embedding_activity):
    content_embeddings = embedding_activity.astype(jnp.float32)
    row_mean = jnp.mean(content_embeddings, axis=-1, keepdims=True)
    centred = content_embeddings - row_mean
    row_var = jnp.mean(centred * centred, axis=-1, keepdims=True)
    return (centred * lax.rsqrt(row_var + epsilon)).astype(jnp.bfloat16)


def block_attention_kernel(sharp_ref, key_ref, value_ref, out_ref, total_ref):
    scale = sharp_ref[pl.program_id(1)]
    n_blocks = out_ref.shape[1] // BLOCK
    rows = lax.broadcasted_iota(jnp.int32, (BLOCK, 2 * BLOCK), 0)
    cols = lax.broadcasted_iota(jnp.int32, (BLOCK, 2 * BLOCK), 1)
    allowed = cols != rows + BLOCK
    for b in range(n_blocks):
        queries = key_ref[0, BLOCK * (b + 1) : BLOCK * (b + 2), :]
        keys = key_ref[0, BLOCK * b : BLOCK * (b + 2), :]
        values = value_ref[0, BLOCK * b : BLOCK * (b + 2), :]
        scores = lax.dot_general(
            queries, keys, (((1,), (1,)), ((), ())), preferred_element_type=jnp.float32
        ) * scale
        exp_scores = jnp.where(allowed, jnp.exp(scores), 0.0)
        totals = jnp.sum(exp_scores, axis=1, keepdims=True)
        weights = (exp_scores / totals).astype(jnp.bfloat16)
        mixed = jnp.dot(weights, values, preferred_element_type=jnp.float32)
        out_ref[0, BLOCK * b : BLOCK * (b + 1), :] = mixed.astype(out_ref.dtype)
        total_ref[0, 0, BLOCK * b : BLOCK * (b + 1), :] = totals


def block_attention(keys_all, values_all, sharpness, head_dim):
    n_rounds, span_rows, cols = keys_all.shape
    rows_here = span_rows - BLOCK
    heads = cols // head_dim
    n_blocks = rows_here // BLOCK
    flops = n_rounds * heads * n_blocks * 4 * BLOCK * 2 * BLOCK * head_dim
    return pl.pallas_call(
        block_attention_kernel,
        grid=(n_rounds, heads),
        in_specs=[
            pl.BlockSpec(memory_space=pltpu.SMEM),
            pl.BlockSpec((1, span_rows, head_dim), lambda r, h: (r, 0, h)),
            pl.BlockSpec((1, span_rows, head_dim), lambda r, h: (r, 0, h)),
        ],
        out_specs=[
            pl.BlockSpec((1, rows_here, head_dim), lambda r, h: (r, 0, h)),
            pl.BlockSpec((1, 1, rows_here, 1), lambda r, h: (r, h, 0, 0)),
        ],
        out_shape=[
            jax.ShapeDtypeStruct((n_rounds, rows_here, cols), jnp.bfloat16),
            jax.ShapeDtypeStruct((n_rounds, heads, rows_here, 1), jnp.float32),
        ],
        cost_estimate=pl.CostEstimate(
            flops=flops,
            transcendentals=n_rounds * heads * n_blocks * BLOCK * 2 * BLOCK,
            bytes_accessed=2 * keys_all.size * 2 + n_rounds * rows_here * cols * 2,
        ),
    )(sharpness, keys_all, values_all)


def rank_within_group(group, order):
    same = group[:, :, None] == group[:, None, :]
    earlier = order[:, None, :] < order[:, :, None]
    return jnp.sum((same & earlier).astype(jnp.int32), axis=2)


def one_hot_rows(index, count):
    return (index[:, :, None] == jnp.arange(count, dtype=jnp.int32)[None, None, :]).astype(
        jnp.bfloat16
    )


def shards(
    embedding_activity,
    common_lookup_projector,
    content_projector,
    final_projector,
    lane_sharpness,
    sorted_place_per_element,
    element_per_sorted_place,
):
    n_dev = lax.axis_size("span")
    rows_here = embedding_activity.shape[0]
    capacity = 2 * rows_here // n_dev
    n_rounds = sorted_place_per_element.shape[0]
    per_peer = n_rounds * capacity
    buffer_rows = n_dev * per_peer
    head_cols = common_lookup_projector.shape[1]
    heads_here = head_cols // HEAD_DIM
    blocks_here = rows_here // BLOCK
    round_ids = jnp.arange(n_rounds, dtype=jnp.int32)[:, None]
    local_ids = jnp.broadcast_to(
        jnp.arange(rows_here, dtype=jnp.int32)[None, :], (n_rounds, rows_here)
    )

    target = sorted_place_per_element // rows_here
    send_rank = rank_within_group(target, local_ids)
    send_row = target * per_peer + round_ids * capacity + send_rank
    send_hot = one_hot_rows(send_row, buffer_rows)

    source = element_per_sorted_place // rows_here
    within = element_per_sorted_place % rows_here
    recv_rank = rank_within_group(source, within)
    recv_row = source * per_peer + round_ids * capacity + recv_rank
    recv_hot = one_hot_rows(recv_row, buffer_rows)

    outgoing = jnp.einsum(
        "rtq,tf->qf", send_hot, embedding_activity, preferred_element_type=jnp.float32
    ).astype(jnp.bfloat16)
    incoming = lax.all_to_all(outgoing, "span", split_axis=0, concat_axis=0, tiled=True)
    arrived = jnp.einsum(
        "rsq,qf->rsf", recv_hot, incoming, preferred_element_type=jnp.float32
    ).astype(jnp.bfloat16)
    n_groups = lax.axis_size("head")
    joined = jnp.concatenate([common_lookup_projector, content_projector], axis=1)
    copies = jnp.broadcast_to(arrived[None], (n_groups,) + arrived.shape)
    gathered = lax.all_to_all(copies, "head", split_axis=0, concat_axis=0, tiled=True)
    last_slice = arrived[:, rows_here - BLOCK :]
    received = []
    for shift in range(n_groups):
        route = [
            (s * n_groups + g, ((s + 1) % n_dev) * n_groups + (g + shift) % n_groups)
            for s in range(n_dev)
            for g in range(n_groups)
        ]
        received.append(lax.ppermute(last_slice, ("span", "head"), route))
    received, gathered = lax.optimization_barrier((received, gathered))
    group_here = lax.axis_index("head")
    slice_order = (group_here - jnp.arange(n_groups, dtype=jnp.int32)) % n_groups
    prior_slices = jnp.take(jnp.stack(received), slice_order, axis=0)
    all_slices = jnp.concatenate([prior_slices, gathered], axis=2)
    span_rows = rows_here + BLOCK
    full_rows = jnp.moveaxis(all_slices, 0, 2).reshape(n_rounds, span_rows, -1)
    normed = layer_norm(full_rows)
    both = jnp.einsum(
        "rsf,fw->rsw", normed, joined, preferred_element_type=jnp.float32
    ).astype(jnp.bfloat16)
    spread = both[:, :, :head_cols].reshape(n_rounds, span_rows, heads_here, HEAD_DIM)
    spread = spread.astype(jnp.float32)
    unitlength_address_lines = (
        spread * lax.rsqrt(jnp.sum(spread * spread, axis=-1, keepdims=True) + 1e-06)
    ).astype(jnp.bfloat16).reshape(n_rounds, span_rows, head_cols)
    sorted_values = both[:, :, head_cols:]
    results, block_totals = block_attention(
        unitlength_address_lines, sorted_values, lane_sharpness, HEAD_DIM
    )
    slot_totals = jnp.transpose(block_totals[..., 0], (0, 2, 1))
    totals_high = slot_totals.astype(jnp.bfloat16)
    totals_low = (slot_totals - totals_high.astype(jnp.float32)).astype(jnp.bfloat16)
    back_payload = jnp.concatenate([results, totals_high, totals_low], axis=2)

    back = jnp.einsum(
        "rsq,rsw->qw", recv_hot, back_payload, preferred_element_type=jnp.float32
    ).astype(jnp.bfloat16)
    home = lax.all_to_all(back, "span", split_axis=0, concat_axis=0, tiled=True)
    token_all = jnp.einsum("rtq,qw->rtw", send_hot, home, preferred_element_type=jnp.float32)
    token_rows = token_all[:, :, :head_cols]
    token_totals = (
        token_all[:, :, head_cols : head_cols + heads_here]
        + token_all[:, :, head_cols + heads_here : head_cols + 2 * heads_here]
    )
    round_share = token_totals / jnp.sum(token_totals, axis=0)
    token_spread = token_rows.reshape(n_rounds, rows_here, heads_here, HEAD_DIM)
    combined = jnp.sum(round_share[..., None] * token_spread, axis=0).astype(jnp.bfloat16)
    combined = combined.reshape(rows_here, head_cols)
    group_part = jnp.dot(
        combined, final_projector, preferred_element_type=jnp.float32
    ).astype(jnp.bfloat16)
    group_parts = lax.all_to_all(
        group_part.reshape(n_groups, rows_here // n_groups, group_part.shape[1]),
        "head",
        split_axis=0,
        concat_axis=0,
        tiled=True,
    )
    return jnp.sum(group_parts.astype(jnp.float32), axis=0).astype(jnp.bfloat16)


def solution(mesh):
    placed = (
        P("span", "head"),
        P(None, "head"),
        P(None, "head"),
        P("head", None),
        P("head"),
        P(None, "span"),
        P(None, "span"),
    )
    return jax.shard_map(
        shards, mesh=mesh, in_specs=placed, out_specs=P(("span", "head"), None), check_vma=False
    )
```

```python
import jax
import jax.numpy as jnp
from jax import lax
from jax.experimental import pallas as pl
from jax.experimental.pallas import tpu as pltpu
from jax.sharding import PartitionSpec as P

HEAD_DIM = 128
BLOCK = 128


epsilon = 1e-05


def passed_along(block, axis, distance):
    devices = range(lax.axis_size(axis))
    route = [((i - distance) % len(devices), i) for i in devices]
    return lax.ppermute(block, axis, route)


def layer_norm(embedding_activity):
    content_embeddings = embedding_activity.astype(jnp.float32)
    row_mean = jnp.mean(content_embeddings, axis=-1, keepdims=True)
    centred = content_embeddings - row_mean
    row_var = jnp.mean(centred * centred, axis=-1, keepdims=True)
    return (centred * lax.rsqrt(row_var + epsilon)).astype(jnp.bfloat16)


def block_attention_kernel(sharp_ref, shared_ref, value_ref, out_ref, total_ref):
    scale = sharp_ref[pl.program_id(1)]
    n_blocks = out_ref.shape[1] // BLOCK
    spread = shared_ref[0].astype(jnp.float32)
    unit = (
        spread * lax.rsqrt(jnp.sum(spread * spread, axis=1, keepdims=True) + 1e-06)
    ).astype(jnp.bfloat16)
    rows = lax.broadcasted_iota(jnp.int32, (BLOCK, 2 * BLOCK), 0)
    cols = lax.broadcasted_iota(jnp.int32, (BLOCK, 2 * BLOCK), 1)
    allowed = cols != rows + BLOCK
    for b in range(n_blocks):
        queries = unit[BLOCK * (b + 1) : BLOCK * (b + 2)]
        keys = unit[BLOCK * b : BLOCK * (b + 2)]
        values = value_ref[0, BLOCK * b : BLOCK * (b + 2), :]
        scores = lax.dot_general(
            queries, keys, (((1,), (1,)), ((), ())), preferred_element_type=jnp.float32
        ) * scale
        exp_scores = jnp.where(allowed, jnp.exp(scores), 0.0)
        totals = jnp.sum(exp_scores, axis=1, keepdims=True)
        weights = (exp_scores / totals).astype(jnp.bfloat16)
        mixed = jnp.dot(weights, values, preferred_element_type=jnp.float32)
        out_ref[0, BLOCK * b : BLOCK * (b + 1), :] = mixed.astype(out_ref.dtype)
        total_ref[0, 0, b : b + 1, :] = jnp.transpose(jnp.broadcast_to(totals, (BLOCK, BLOCK)))[0:1]


def block_attention(both, sharpness, head_dim):
    n_rounds, span_rows, cols = both.shape
    rows_here = span_rows - BLOCK
    heads = cols // (2 * head_dim)
    n_blocks = rows_here // BLOCK
    flops = n_rounds * heads * n_blocks * 4 * BLOCK * 2 * BLOCK * head_dim
    return pl.pallas_call(
        block_attention_kernel,
        grid=(n_rounds, heads),
        in_specs=[
            pl.BlockSpec(memory_space=pltpu.SMEM),
            pl.BlockSpec((1, span_rows, head_dim), lambda r, h: (r, 0, h)),
            pl.BlockSpec((1, span_rows, head_dim), lambda r, h: (r, 0, heads + h)),
        ],
        out_specs=[
            pl.BlockSpec((1, rows_here, head_dim), lambda r, h: (r, 0, h)),
            pl.BlockSpec((1, 1, n_blocks, BLOCK), lambda r, h: (r, h, 0, 0)),
        ],
        out_shape=[
            jax.ShapeDtypeStruct((n_rounds, rows_here, heads * head_dim), jnp.bfloat16),
            jax.ShapeDtypeStruct((n_rounds, heads, n_blocks, BLOCK), jnp.float32),
        ],
        cost_estimate=pl.CostEstimate(
            flops=flops,
            transcendentals=n_rounds * heads * n_blocks * BLOCK * 2 * BLOCK,
            bytes_accessed=both.size * 2 + n_rounds * rows_here * heads * head_dim * 2,
        ),
    )(sharpness, both, both)


def rank_within_group(group, order):
    same = group[:, :, None] == group[:, None, :]
    earlier = order[:, None, :] < order[:, :, None]
    return jnp.sum((same & earlier).astype(jnp.int32), axis=2)


def one_hot_rows(index, count):
    return (index[:, :, None] == jnp.arange(count, dtype=jnp.int32)[None, None, :]).astype(
        jnp.bfloat16
    )


def shards(
    embedding_activity,
    common_lookup_projector,
    content_projector,
    final_projector,
    lane_sharpness,
    sorted_place_per_element,
    element_per_sorted_place,
):
    n_dev = lax.axis_size("span")
    rows_here = embedding_activity.shape[0]
    capacity = 2 * rows_here // n_dev
    n_rounds = sorted_place_per_element.shape[0]
    per_peer = n_rounds * capacity
    buffer_rows = n_dev * per_peer
    head_cols = common_lookup_projector.shape[1]
    heads_here = head_cols // HEAD_DIM
    blocks_here = rows_here // BLOCK
    round_ids = jnp.arange(n_rounds, dtype=jnp.int32)[:, None]
    local_ids = jnp.broadcast_to(
        jnp.arange(rows_here, dtype=jnp.int32)[None, :], (n_rounds, rows_here)
    )

    target = sorted_place_per_element // rows_here
    send_rank = rank_within_group(target, local_ids)
    send_row = target * per_peer + round_ids * capacity + send_rank
    send_hot = one_hot_rows(send_row, buffer_rows)

    source = element_per_sorted_place // rows_here
    within = element_per_sorted_place % rows_here
    recv_rank = rank_within_group(source, within)
    recv_row = source * per_peer + round_ids * capacity + recv_rank
    recv_hot = one_hot_rows(recv_row, buffer_rows)

    outgoing = jnp.einsum(
        "rtq,tf->qf", send_hot, embedding_activity, preferred_element_type=jnp.float32
    ).astype(jnp.bfloat16)
    incoming = lax.all_to_all(outgoing, "span", split_axis=0, concat_axis=0, tiled=True)
    arrived = jnp.einsum(
        "rsq,qf->rsf", recv_hot, incoming, preferred_element_type=jnp.float32
    ).astype(jnp.bfloat16)
    n_groups = lax.axis_size("head")
    joined = jnp.concatenate([common_lookup_projector, content_projector], axis=1)
    copies = jnp.broadcast_to(arrived[None], (n_groups,) + arrived.shape)
    gathered = lax.all_to_all(copies, "head", split_axis=0, concat_axis=0, tiled=True)
    last_slice = arrived[:, rows_here - BLOCK :]
    received = []
    for shift in range(n_groups):
        route = [
            (s * n_groups + g, ((s + 1) % n_dev) * n_groups + (g + shift) % n_groups)
            for s in range(n_dev)
            for g in range(n_groups)
        ]
        received.append(lax.ppermute(last_slice, ("span", "head"), route))
    received, gathered = lax.optimization_barrier((received, gathered))
    group_here = lax.axis_index("head")
    slice_order = (group_here - jnp.arange(n_groups, dtype=jnp.int32)) % n_groups
    prior_slices = jnp.take(jnp.stack(received), slice_order, axis=0)
    all_slices = jnp.concatenate([prior_slices, gathered], axis=2)
    span_rows = rows_here + BLOCK
    full_rows = jnp.moveaxis(all_slices, 0, 2).reshape(n_rounds, span_rows, -1)
    normed = layer_norm(full_rows)
    both = jnp.einsum(
        "rsf,fw->rsw", normed, joined, preferred_element_type=jnp.float32
    ).astype(jnp.bfloat16)
    results, block_totals = block_attention(both, lane_sharpness, HEAD_DIM)
    slot_totals = jnp.transpose(
        block_totals.reshape(n_rounds, heads_here, rows_here), (0, 2, 1)
    )
    totals_high = slot_totals.astype(jnp.bfloat16)
    totals_low = (slot_totals - totals_high.astype(jnp.float32)).astype(jnp.bfloat16)
    back_payload = jnp.concatenate([results, totals_high, totals_low], axis=2)

    back = jnp.einsum(
        "rsq,rsw->qw", recv_hot, back_payload, preferred_element_type=jnp.float32
    ).astype(jnp.bfloat16)
    home = lax.all_to_all(back, "span", split_axis=0, concat_axis=0, tiled=True)
    token_all = jnp.einsum("rtq,qw->rtw", send_hot, home, preferred_element_type=jnp.float32)
    token_rows = token_all[:, :, :head_cols]
    token_totals = (
        token_all[:, :, head_cols : head_cols + heads_here]
        + token_all[:, :, head_cols + heads_here : head_cols + 2 * heads_here]
    )
    round_share = token_totals / jnp.sum(token_totals, axis=0)
    token_spread = token_rows.reshape(n_rounds, rows_here, heads_here, HEAD_DIM)
    combined = jnp.sum(round_share[..., None] * token_spread, axis=0).astype(jnp.bfloat16)
    combined = combined.reshape(rows_here, head_cols)
    group_part = jnp.dot(
        combined, final_projector, preferred_element_type=jnp.float32
    ).astype(jnp.bfloat16)
    group_parts = lax.all_to_all(
        group_part.reshape(n_groups, rows_here // n_groups, group_part.shape[1]),
        "head",
        split_axis=0,
        concat_axis=0,
        tiled=True,
    )
    return jnp.sum(group_parts.astype(jnp.float32), axis=0).astype(jnp.bfloat16)


def solution(mesh):
    placed = (
        P("span", "head"),
        P(None, "head"),
        P(None, "head"),
        P("head", None),
        P("head"),
        P(None, "span"),
        P(None, "span"),
    )
    return jax.shard_map(
        shards, mesh=mesh, in_specs=placed, out_specs=P(("span", "head"), None), check_vma=False
    )
```

```python
import jax
import jax.numpy as jnp
from jax import lax
from jax.experimental import pallas as pl
from jax.experimental.pallas import tpu as pltpu
from jax.sharding import PartitionSpec as P

HEAD_DIM = 128
BLOCK = 128


epsilon = 1e-05


def passed_along(block, axis, distance):
    devices = range(lax.axis_size(axis))
    route = [((i - distance) % len(devices), i) for i in devices]
    return lax.ppermute(block, axis, route)


def layer_norm(embedding_activity):
    content_embeddings = embedding_activity.astype(jnp.float32)
    row_mean = jnp.mean(content_embeddings, axis=-1, keepdims=True)
    centred = content_embeddings - row_mean
    row_var = jnp.mean(centred * centred, axis=-1, keepdims=True)
    return (centred * lax.rsqrt(row_var + epsilon)).astype(jnp.bfloat16)


def block_attention_kernel(sharp_ref, both_ref, out_ref, total_ref):
    n_rounds, span_rows, cols = both_ref.shape
    heads = out_ref.shape[2] // HEAD_DIM
    n_blocks = out_ref.shape[1] // BLOCK
    rows = lax.broadcasted_iota(jnp.int32, (BLOCK, 2 * BLOCK), 0)
    key_cols = lax.broadcasted_iota(jnp.int32, (BLOCK, 2 * BLOCK), 1)
    allowed = key_cols != rows + BLOCK
    for r in range(n_rounds):
        for h in range(heads):
            scale = sharp_ref[h]
            spread = both_ref[r, :, HEAD_DIM * h : HEAD_DIM * (h + 1)].astype(jnp.float32)
            unit = (
                spread * lax.rsqrt(jnp.sum(spread * spread, axis=1, keepdims=True) + 1e-06)
            ).astype(jnp.bfloat16)
            value_col = HEAD_DIM * (heads + h)
            for b in range(n_blocks):
                queries = unit[BLOCK * (b + 1) : BLOCK * (b + 2)]
                keys = unit[BLOCK * b : BLOCK * (b + 2)]
                values = both_ref[r, BLOCK * b : BLOCK * (b + 2), value_col : value_col + HEAD_DIM]
                scores = lax.dot_general(
                    queries, keys, (((1,), (1,)), ((), ())), preferred_element_type=jnp.float32
                ) * scale
                exp_scores = jnp.where(allowed, jnp.exp(scores), 0.0)
                totals = jnp.sum(exp_scores, axis=1, keepdims=True)
                weights = (exp_scores / totals).astype(jnp.bfloat16)
                mixed = jnp.dot(weights, values, preferred_element_type=jnp.float32)
                out_ref[r, BLOCK * b : BLOCK * (b + 1), HEAD_DIM * h : HEAD_DIM * (h + 1)] = (
                    mixed.astype(out_ref.dtype)
                )
                total_ref[r, h, b : b + 1, :] = jnp.transpose(
                    jnp.broadcast_to(totals, (BLOCK, BLOCK))
                )[0:1]


def block_attention(both, sharpness, head_dim):
    n_rounds, span_rows, cols = both.shape
    rows_here = span_rows - BLOCK
    heads = cols // (2 * head_dim)
    n_blocks = rows_here // BLOCK
    flops = n_rounds * heads * n_blocks * 4 * BLOCK * 2 * BLOCK * head_dim
    return pl.pallas_call(
        block_attention_kernel,
        in_specs=[
            pl.BlockSpec(memory_space=pltpu.SMEM),
            pl.BlockSpec(memory_space=pltpu.VMEM),
        ],
        out_specs=[
            pl.BlockSpec(memory_space=pltpu.VMEM),
            pl.BlockSpec(memory_space=pltpu.VMEM),
        ],
        out_shape=[
            jax.ShapeDtypeStruct((n_rounds, rows_here, heads * head_dim), jnp.bfloat16),
            jax.ShapeDtypeStruct((n_rounds, heads, n_blocks, BLOCK), jnp.float32),
        ],
        cost_estimate=pl.CostEstimate(
            flops=flops,
            transcendentals=n_rounds * heads * n_blocks * BLOCK * 2 * BLOCK,
            bytes_accessed=both.size * 2 + n_rounds * rows_here * heads * head_dim * 2,
        ),
    )(sharpness, both)


def rank_within_group(group, order):
    same = group[:, :, None] == group[:, None, :]
    earlier = order[:, None, :] < order[:, :, None]
    return jnp.sum((same & earlier).astype(jnp.int32), axis=2)


def one_hot_rows(index, count):
    return (index[:, :, None] == jnp.arange(count, dtype=jnp.int32)[None, None, :]).astype(
        jnp.bfloat16
    )


def shards(
    embedding_activity,
    common_lookup_projector,
    content_projector,
    final_projector,
    lane_sharpness,
    sorted_place_per_element,
    element_per_sorted_place,
):
    n_dev = lax.axis_size("span")
    rows_here = embedding_activity.shape[0]
    capacity = 2 * rows_here // n_dev
    n_rounds = sorted_place_per_element.shape[0]
    per_peer = n_rounds * capacity
    buffer_rows = n_dev * per_peer
    head_cols = common_lookup_projector.shape[1]
    heads_here = head_cols // HEAD_DIM
    blocks_here = rows_here // BLOCK
    round_ids = jnp.arange(n_rounds, dtype=jnp.int32)[:, None]
    local_ids = jnp.broadcast_to(
        jnp.arange(rows_here, dtype=jnp.int32)[None, :], (n_rounds, rows_here)
    )

    target = sorted_place_per_element // rows_here
    send_rank = rank_within_group(target, local_ids)
    send_row = target * per_peer + round_ids * capacity + send_rank
    send_hot = one_hot_rows(send_row, buffer_rows)

    source = element_per_sorted_place // rows_here
    within = element_per_sorted_place % rows_here
    recv_rank = rank_within_group(source, within)
    recv_row = source * per_peer + round_ids * capacity + recv_rank
    recv_hot = one_hot_rows(recv_row, buffer_rows)

    outgoing = jnp.einsum(
        "rtq,tf->qf", send_hot, embedding_activity, preferred_element_type=jnp.float32
    ).astype(jnp.bfloat16)
    incoming = lax.all_to_all(outgoing, "span", split_axis=0, concat_axis=0, tiled=True)
    arrived = jnp.einsum(
        "rsq,qf->rsf", recv_hot, incoming, preferred_element_type=jnp.float32
    ).astype(jnp.bfloat16)
    n_groups = lax.axis_size("head")
    joined = jnp.concatenate([common_lookup_projector, content_projector], axis=1)
    copies = jnp.broadcast_to(arrived[None], (n_groups,) + arrived.shape)
    gathered = lax.all_to_all(copies, "head", split_axis=0, concat_axis=0, tiled=True)
    last_slice = arrived[:, rows_here - BLOCK :]
    received = []
    for shift in range(n_groups):
        route = [
            (s * n_groups + g, ((s + 1) % n_dev) * n_groups + (g + shift) % n_groups)
            for s in range(n_dev)
            for g in range(n_groups)
        ]
        received.append(lax.ppermute(last_slice, ("span", "head"), route))
    received, gathered = lax.optimization_barrier((received, gathered))
    group_here = lax.axis_index("head")
    slice_order = (group_here - jnp.arange(n_groups, dtype=jnp.int32)) % n_groups
    prior_slices = jnp.take(jnp.stack(received), slice_order, axis=0)
    all_slices = jnp.concatenate([prior_slices, gathered], axis=2)
    span_rows = rows_here + BLOCK
    full_rows = jnp.moveaxis(all_slices, 0, 2).reshape(n_rounds, span_rows, -1)
    normed = layer_norm(full_rows)
    both = jnp.einsum(
        "rsf,fw->rsw", normed, joined, preferred_element_type=jnp.float32
    ).astype(jnp.bfloat16)
    results, block_totals = block_attention(both, lane_sharpness, HEAD_DIM)
    slot_totals = jnp.transpose(
        block_totals.reshape(n_rounds, heads_here, rows_here), (0, 2, 1)
    )
    totals_high = slot_totals.astype(jnp.bfloat16)
    totals_low = (slot_totals - totals_high.astype(jnp.float32)).astype(jnp.bfloat16)
    back_payload = jnp.concatenate([results, totals_high, totals_low], axis=2)

    back = jnp.einsum(
        "rsq,rsw->qw", recv_hot, back_payload, preferred_element_type=jnp.float32
    ).astype(jnp.bfloat16)
    home = lax.all_to_all(back, "span", split_axis=0, concat_axis=0, tiled=True)
    token_all = jnp.einsum("rtq,qw->rtw", send_hot, home, preferred_element_type=jnp.float32)
    token_rows = token_all[:, :, :head_cols]
    token_totals = (
        token_all[:, :, head_cols : head_cols + heads_here]
        + token_all[:, :, head_cols + heads_here : head_cols + 2 * heads_here]
    )
    round_share = token_totals / jnp.sum(token_totals, axis=0)
    token_spread = token_rows.reshape(n_rounds, rows_here, heads_here, HEAD_DIM)
    combined = jnp.sum(round_share[..., None] * token_spread, axis=0).astype(jnp.bfloat16)
    combined = combined.reshape(rows_here, head_cols)
    group_part = jnp.dot(
        combined, final_projector, preferred_element_type=jnp.float32
    ).astype(jnp.bfloat16)
    group_parts = lax.all_to_all(
        group_part.reshape(n_groups, rows_here // n_groups, group_part.shape[1]),
        "head",
        split_axis=0,
        concat_axis=0,
        tiled=True,
    )
    return jnp.sum(group_parts.astype(jnp.float32), axis=0).astype(jnp.bfloat16)


def solution(mesh):
    placed = (
        P("span", "head"),
        P(None, "head"),
        P(None, "head"),
        P("head", None),
        P("head"),
        P(None, "span"),
        P(None, "span"),
    )
    return jax.shard_map(
        shards, mesh=mesh, in_specs=placed, out_specs=P(("span", "head"), None), check_vma=False
    )
```

```python
import jax
import jax.numpy as jnp
from jax import lax
from jax.experimental import pallas as pl
from jax.experimental.pallas import tpu as pltpu
from jax.sharding import PartitionSpec as P

HEAD_DIM = 128
BLOCK = 128


epsilon = 1e-05


def passed_along(block, axis, distance):
    devices = range(lax.axis_size(axis))
    route = [((i - distance) % len(devices), i) for i in devices]
    return lax.ppermute(block, axis, route)


def layer_norm(embedding_activity):
    content_embeddings = embedding_activity.astype(jnp.float32)
    row_mean = jnp.mean(content_embeddings, axis=-1, keepdims=True)
    centred = content_embeddings - row_mean
    row_var = jnp.mean(centred * centred, axis=-1, keepdims=True)
    return (centred * lax.rsqrt(row_var + epsilon)).astype(jnp.bfloat16)


def block_attention_kernel(
    sharp_ref, slices_ref, shared_proj_ref, value_proj_ref, out_ref, total_ref
):
    n_groups, n_rounds, span_rows, group_cols = slices_ref.shape
    heads = out_ref.shape[2] // HEAD_DIM
    n_blocks = out_ref.shape[1] // BLOCK
    features = n_groups * group_cols
    rows = lax.broadcasted_iota(jnp.int32, (BLOCK, 2 * BLOCK), 0)
    key_cols = lax.broadcasted_iota(jnp.int32, (BLOCK, 2 * BLOCK), 1)
    allowed = key_cols != rows + BLOCK
    for r in range(n_rounds):
        parts = [slices_ref[g, r].astype(jnp.float32) for g in range(n_groups)]
        row_mean = sum(jnp.sum(p, axis=1, keepdims=True) for p in parts) / features
        centred = [p - row_mean for p in parts]
        row_var = sum(jnp.sum(c * c, axis=1, keepdims=True) for c in centred) / features
        inv = lax.rsqrt(row_var + epsilon)
        normed = [(c * inv).astype(jnp.bfloat16) for c in centred]
        projected = []
        for proj_ref in (shared_proj_ref, value_proj_ref):
            acc = None
            for g in range(n_groups):
                term = jnp.dot(
                    normed[g],
                    proj_ref[group_cols * g : group_cols * (g + 1), :],
                    preferred_element_type=jnp.float32,
                )
                acc = term if acc is None else acc + term
            projected.append(acc.astype(jnp.bfloat16))
        shared, values_all = projected
        for h in range(heads):
            scale = sharp_ref[h]
            spread = shared[:, HEAD_DIM * h : HEAD_DIM * (h + 1)].astype(jnp.float32)
            unit = (
                spread * lax.rsqrt(jnp.sum(spread * spread, axis=1, keepdims=True) + 1e-06)
            ).astype(jnp.bfloat16)
            for b in range(n_blocks):
                queries = unit[BLOCK * (b + 1) : BLOCK * (b + 2)]
                keys = unit[BLOCK * b : BLOCK * (b + 2)]
                values = values_all[BLOCK * b : BLOCK * (b + 2), HEAD_DIM * h : HEAD_DIM * (h + 1)]
                scores = lax.dot_general(
                    queries, keys, (((1,), (1,)), ((), ())), preferred_element_type=jnp.float32
                ) * scale
                exp_scores = jnp.where(allowed, jnp.exp(scores), 0.0)
                totals = jnp.sum(exp_scores, axis=1, keepdims=True)
                weights = (exp_scores / totals).astype(jnp.bfloat16)
                mixed = jnp.dot(weights, values, preferred_element_type=jnp.float32)
                out_ref[r, BLOCK * b : BLOCK * (b + 1), HEAD_DIM * h : HEAD_DIM * (h + 1)] = (
                    mixed.astype(out_ref.dtype)
                )
                total_ref[r, h, b : b + 1, :] = jnp.transpose(
                    jnp.broadcast_to(totals, (BLOCK, BLOCK))
                )[0:1]


def block_attention(slices, shared_proj, value_proj, sharpness):
    n_groups, n_rounds, span_rows, group_cols = slices.shape
    rows_here = span_rows - BLOCK
    cols = shared_proj.shape[1]
    heads = cols // HEAD_DIM
    n_blocks = rows_here // BLOCK
    flops = n_rounds * heads * n_blocks * 4 * BLOCK * 2 * BLOCK * HEAD_DIM
    flops += n_rounds * span_rows * n_groups * group_cols * 2 * cols * 2
    vmem = pl.BlockSpec(memory_space=pltpu.VMEM)
    return pl.pallas_call(
        block_attention_kernel,
        in_specs=[pl.BlockSpec(memory_space=pltpu.SMEM), vmem, vmem, vmem],
        out_specs=[vmem, vmem],
        out_shape=[
            jax.ShapeDtypeStruct((n_rounds, rows_here, cols), jnp.bfloat16),
            jax.ShapeDtypeStruct((n_rounds, heads, n_blocks, BLOCK), jnp.float32),
        ],
        cost_estimate=pl.CostEstimate(
            flops=flops,
            transcendentals=n_rounds * heads * n_blocks * BLOCK * 2 * BLOCK,
            bytes_accessed=slices.size * 2 + 4 * shared_proj.size + n_rounds * rows_here * cols * 2,
        ),
    )(sharpness, slices, shared_proj, value_proj)


def rank_within_group(group, order):
    same = group[:, :, None] == group[:, None, :]
    earlier = order[:, None, :] < order[:, :, None]
    return jnp.sum((same & earlier).astype(jnp.int32), axis=2)


def one_hot_rows(index, count):
    return (index[:, :, None] == jnp.arange(count, dtype=jnp.int32)[None, None, :]).astype(
        jnp.bfloat16
    )


def shards(
    embedding_activity,
    common_lookup_projector,
    content_projector,
    final_projector,
    lane_sharpness,
    sorted_place_per_element,
    element_per_sorted_place,
):
    n_dev = lax.axis_size("span")
    rows_here = embedding_activity.shape[0]
    capacity = 2 * rows_here // n_dev
    n_rounds = sorted_place_per_element.shape[0]
    per_peer = n_rounds * capacity
    buffer_rows = n_dev * per_peer
    head_cols = common_lookup_projector.shape[1]
    heads_here = head_cols // HEAD_DIM
    blocks_here = rows_here // BLOCK
    round_ids = jnp.arange(n_rounds, dtype=jnp.int32)[:, None]
    local_ids = jnp.broadcast_to(
        jnp.arange(rows_here, dtype=jnp.int32)[None, :], (n_rounds, rows_here)
    )

    target = sorted_place_per_element // rows_here
    send_rank = rank_within_group(target, local_ids)
    send_row = target * per_peer + round_ids * capacity + send_rank
    send_hot = one_hot_rows(send_row, buffer_rows)

    source = element_per_sorted_place // rows_here
    within = element_per_sorted_place % rows_here
    recv_rank = rank_within_group(source, within)
    recv_row = source * per_peer + round_ids * capacity + recv_rank
    recv_hot = one_hot_rows(recv_row, buffer_rows)

    outgoing = jnp.einsum(
        "rtq,tf->qf", send_hot, embedding_activity, preferred_element_type=jnp.float32
    ).astype(jnp.bfloat16)
    incoming = lax.all_to_all(outgoing, "span", split_axis=0, concat_axis=0, tiled=True)
    arrived = jnp.einsum(
        "rsq,qf->rsf", recv_hot, incoming, preferred_element_type=jnp.float32
    ).astype(jnp.bfloat16)
    n_groups = lax.axis_size("head")
    copies = jnp.broadcast_to(arrived[None], (n_groups,) + arrived.shape)
    gathered = lax.all_to_all(copies, "head", split_axis=0, concat_axis=0, tiled=True)
    last_slice = arrived[:, rows_here - BLOCK :]
    received = []
    for shift in range(n_groups):
        route = [
            (s * n_groups + g, ((s + 1) % n_dev) * n_groups + (g + shift) % n_groups)
            for s in range(n_dev)
            for g in range(n_groups)
        ]
        received.append(lax.ppermute(last_slice, ("span", "head"), route))
    received, gathered = lax.optimization_barrier((received, gathered))
    group_here = lax.axis_index("head")
    slice_order = (group_here - jnp.arange(n_groups, dtype=jnp.int32)) % n_groups
    prior_slices = jnp.take(jnp.stack(received), slice_order, axis=0)
    all_slices = jnp.concatenate([prior_slices, gathered], axis=2)
    results, block_totals = block_attention(
        all_slices, common_lookup_projector, content_projector, lane_sharpness
    )
    slot_totals = jnp.transpose(
        block_totals.reshape(n_rounds, heads_here, rows_here), (0, 2, 1)
    )
    totals_high = slot_totals.astype(jnp.bfloat16)
    totals_low = (slot_totals - totals_high.astype(jnp.float32)).astype(jnp.bfloat16)
    back_payload = jnp.concatenate([results, totals_high, totals_low], axis=2)

    back = jnp.einsum(
        "rsq,rsw->qw", recv_hot, back_payload, preferred_element_type=jnp.float32
    ).astype(jnp.bfloat16)
    home = lax.all_to_all(back, "span", split_axis=0, concat_axis=0, tiled=True)
    token_all = jnp.einsum("rtq,qw->rtw", send_hot, home, preferred_element_type=jnp.float32)
    token_rows = token_all[:, :, :head_cols]
    token_totals = (
        token_all[:, :, head_cols : head_cols + heads_here]
        + token_all[:, :, head_cols + heads_here : head_cols + 2 * heads_here]
    )
    round_share = token_totals / jnp.sum(token_totals, axis=0)
    token_spread = token_rows.reshape(n_rounds, rows_here, heads_here, HEAD_DIM)
    combined = jnp.sum(round_share[..., None] * token_spread, axis=0).astype(jnp.bfloat16)
    combined = combined.reshape(rows_here, head_cols)
    group_part = jnp.dot(
        combined, final_projector, preferred_element_type=jnp.float32
    ).astype(jnp.bfloat16)
    group_parts = lax.all_to_all(
        group_part.reshape(n_groups, rows_here // n_groups, group_part.shape[1]),
        "head",
        split_axis=0,
        concat_axis=0,
        tiled=True,
    )
    return jnp.sum(group_parts.astype(jnp.float32), axis=0).astype(jnp.bfloat16)


def solution(mesh):
    placed = (
        P("span", "head"),
        P(None, "head"),
        P(None, "head"),
        P("head", None),
        P("head"),
        P(None, "span"),
        P(None, "span"),
    )
    return jax.shard_map(
        shards, mesh=mesh, in_specs=placed, out_specs=P(("span", "head"), None), check_vma=False
    )
```

```python
import jax
import jax.numpy as jnp
from jax import lax
from jax.experimental import pallas as pl
from jax.experimental.pallas import tpu as pltpu
from jax.sharding import PartitionSpec as P

HEAD_DIM = 128
BLOCK = 128


epsilon = 1e-05


def passed_along(block, axis, distance):
    devices = range(lax.axis_size(axis))
    route = [((i - distance) % len(devices), i) for i in devices]
    return lax.ppermute(block, axis, route)


def layer_norm(embedding_activity):
    content_embeddings = embedding_activity.astype(jnp.float32)
    row_mean = jnp.mean(content_embeddings, axis=-1, keepdims=True)
    centred = content_embeddings - row_mean
    row_var = jnp.mean(centred * centred, axis=-1, keepdims=True)
    return (centred * lax.rsqrt(row_var + epsilon)).astype(jnp.bfloat16)


def block_attention_kernel(
    sharp_ref, order_ref, prior_ref, here_ref, shared_proj_ref, value_proj_ref, out_ref, total_ref
):
    n_groups, n_rounds, rows_here, group_cols = here_ref.shape
    heads = out_ref.shape[2] // HEAD_DIM
    n_blocks = out_ref.shape[1] // BLOCK
    features = n_groups * group_cols
    rows = lax.broadcasted_iota(jnp.int32, (BLOCK, 2 * BLOCK), 0)
    key_cols = lax.broadcasted_iota(jnp.int32, (BLOCK, 2 * BLOCK), 1)
    allowed = key_cols != rows + BLOCK
    for r in range(n_rounds):
        parts = [
            jnp.concatenate([prior_ref[order_ref[g], r], here_ref[g, r]], axis=0).astype(jnp.float32)
            for g in range(n_groups)
        ]
        row_mean = sum(jnp.sum(p, axis=1, keepdims=True) for p in parts) / features
        centred = [p - row_mean for p in parts]
        row_var = sum(jnp.sum(c * c, axis=1, keepdims=True) for c in centred) / features
        inv = lax.rsqrt(row_var + epsilon)
        normed = [(c * inv).astype(jnp.bfloat16) for c in centred]
        projected = []
        for proj_ref in (shared_proj_ref, value_proj_ref):
            acc = None
            for g in range(n_groups):
                term = jnp.dot(
                    normed[g],
                    proj_ref[group_cols * g : group_cols * (g + 1), :],
                    preferred_element_type=jnp.float32,
                )
                acc = term if acc is None else acc + term
            projected.append(acc.astype(jnp.bfloat16))
        shared, values_all = projected
        for h in range(heads):
            scale = sharp_ref[h]
            spread = shared[:, HEAD_DIM * h : HEAD_DIM * (h + 1)].astype(jnp.float32)
            unit = (
                spread * lax.rsqrt(jnp.sum(spread * spread, axis=1, keepdims=True) + 1e-06)
            ).astype(jnp.bfloat16)
            for b in range(n_blocks):
                queries = unit[BLOCK * (b + 1) : BLOCK * (b + 2)]
                keys = unit[BLOCK * b : BLOCK * (b + 2)]
                values = values_all[BLOCK * b : BLOCK * (b + 2), HEAD_DIM * h : HEAD_DIM * (h + 1)]
                scores = lax.dot_general(
                    queries, keys, (((1,), (1,)), ((), ())), preferred_element_type=jnp.float32
                ) * scale
                exp_scores = jnp.where(allowed, jnp.exp(scores), 0.0)
                totals = jnp.sum(exp_scores, axis=1, keepdims=True)
                weights = (exp_scores / totals).astype(jnp.bfloat16)
                mixed = jnp.dot(weights, values, preferred_element_type=jnp.float32)
                out_ref[r, BLOCK * b : BLOCK * (b + 1), HEAD_DIM * h : HEAD_DIM * (h + 1)] = (
                    mixed.astype(out_ref.dtype)
                )
                total_ref[r, h, b : b + 1, :] = jnp.transpose(
                    jnp.broadcast_to(totals, (BLOCK, BLOCK))
                )[0:1]


def block_attention(prior, order, here, shared_proj, value_proj, sharpness):
    n_groups, n_rounds, rows_here, group_cols = here.shape
    span_rows = rows_here + BLOCK
    cols = shared_proj.shape[1]
    heads = cols // HEAD_DIM
    n_blocks = rows_here // BLOCK
    flops = n_rounds * heads * n_blocks * 4 * BLOCK * 2 * BLOCK * HEAD_DIM
    flops += n_rounds * span_rows * n_groups * group_cols * 2 * cols * 2
    vmem = pl.BlockSpec(memory_space=pltpu.VMEM)
    smem = pl.BlockSpec(memory_space=pltpu.SMEM)
    return pl.pallas_call(
        block_attention_kernel,
        in_specs=[smem, smem, vmem, vmem, vmem, vmem],
        out_specs=[vmem, vmem],
        out_shape=[
            jax.ShapeDtypeStruct((n_rounds, rows_here, cols), jnp.bfloat16),
            jax.ShapeDtypeStruct((n_rounds, heads, n_blocks, BLOCK), jnp.float32),
        ],
        cost_estimate=pl.CostEstimate(
            flops=flops,
            transcendentals=n_rounds * heads * n_blocks * BLOCK * 2 * BLOCK,
            bytes_accessed=(prior.size + here.size) * 2 + 4 * shared_proj.size
            + n_rounds * rows_here * cols * 2,
        ),
    )(sharpness, order, prior, here, shared_proj, value_proj)


def rank_within_group(group, order):
    same = group[:, :, None] == group[:, None, :]
    earlier = order[:, None, :] < order[:, :, None]
    return jnp.sum((same & earlier).astype(jnp.int32), axis=2)


def one_hot_rows(index, count):
    return (index[:, :, None] == jnp.arange(count, dtype=jnp.int32)[None, None, :]).astype(
        jnp.bfloat16
    )


def shards(
    embedding_activity,
    common_lookup_projector,
    content_projector,
    final_projector,
    lane_sharpness,
    sorted_place_per_element,
    element_per_sorted_place,
):
    n_dev = lax.axis_size("span")
    rows_here = embedding_activity.shape[0]
    capacity = 2 * rows_here // n_dev
    n_rounds = sorted_place_per_element.shape[0]
    per_peer = n_rounds * capacity
    buffer_rows = n_dev * per_peer
    head_cols = common_lookup_projector.shape[1]
    heads_here = head_cols // HEAD_DIM
    blocks_here = rows_here // BLOCK
    round_ids = jnp.arange(n_rounds, dtype=jnp.int32)[:, None]
    local_ids = jnp.broadcast_to(
        jnp.arange(rows_here, dtype=jnp.int32)[None, :], (n_rounds, rows_here)
    )

    target = sorted_place_per_element // rows_here
    send_rank = rank_within_group(target, local_ids)
    send_row = target * per_peer + round_ids * capacity + send_rank
    send_hot = one_hot_rows(send_row, buffer_rows)

    source = element_per_sorted_place // rows_here
    within = element_per_sorted_place % rows_here
    recv_rank = rank_within_group(source, within)
    recv_row = source * per_peer + round_ids * capacity + recv_rank
    recv_hot = one_hot_rows(recv_row, buffer_rows)

    outgoing = jnp.einsum(
        "rtq,tf->qf", send_hot, embedding_activity, preferred_element_type=jnp.float32
    ).astype(jnp.bfloat16)
    incoming = lax.all_to_all(outgoing, "span", split_axis=0, concat_axis=0, tiled=True)
    arrived = jnp.einsum(
        "rsq,qf->rsf", recv_hot, incoming, preferred_element_type=jnp.float32
    ).astype(jnp.bfloat16)
    n_groups = lax.axis_size("head")
    copies = jnp.broadcast_to(arrived[None], (n_groups,) + arrived.shape)
    gathered = lax.all_to_all(copies, "head", split_axis=0, concat_axis=0, tiled=True)
    last_slice = arrived[:, rows_here - BLOCK :]
    received = []
    for shift in range(n_groups):
        route = [
            (s * n_groups + g, ((s + 1) % n_dev) * n_groups + (g + shift) % n_groups)
            for s in range(n_dev)
            for g in range(n_groups)
        ]
        received.append(lax.ppermute(last_slice, ("span", "head"), route))
    received, gathered = lax.optimization_barrier((received, gathered))
    group_here = lax.axis_index("head")
    slice_order = (group_here - jnp.arange(n_groups, dtype=jnp.int32)) % n_groups
    prior_stack = jnp.stack(received)
    results, block_totals = block_attention(
        prior_stack, slice_order, gathered, common_lookup_projector, content_projector, lane_sharpness
    )
    slot_totals = jnp.transpose(
        block_totals.reshape(n_rounds, heads_here, rows_here), (0, 2, 1)
    )
    totals_high = slot_totals.astype(jnp.bfloat16)
    totals_low = (slot_totals - totals_high.astype(jnp.float32)).astype(jnp.bfloat16)
    back_payload = jnp.concatenate([results, totals_high, totals_low], axis=2)

    back = jnp.einsum(
        "rsq,rsw->qw", recv_hot, back_payload, preferred_element_type=jnp.float32
    ).astype(jnp.bfloat16)
    home = lax.all_to_all(back, "span", split_axis=0, concat_axis=0, tiled=True)
    token_all = jnp.einsum("rtq,qw->rtw", send_hot, home, preferred_element_type=jnp.float32)
    token_rows = token_all[:, :, :head_cols]
    token_totals = (
        token_all[:, :, head_cols : head_cols + heads_here]
        + token_all[:, :, head_cols + heads_here : head_cols + 2 * heads_here]
    )
    round_share = token_totals / jnp.sum(token_totals, axis=0)
    token_spread = token_rows.reshape(n_rounds, rows_here, heads_here, HEAD_DIM)
    combined = jnp.sum(round_share[..., None] * token_spread, axis=0).astype(jnp.bfloat16)
    combined = combined.reshape(rows_here, head_cols)
    group_part = jnp.dot(
        combined, final_projector, preferred_element_type=jnp.float32
    ).astype(jnp.bfloat16)
    group_parts = lax.all_to_all(
        group_part.reshape(n_groups, rows_here // n_groups, group_part.shape[1]),
        "head",
        split_axis=0,
        concat_axis=0,
        tiled=True,
    )
    return jnp.sum(group_parts.astype(jnp.float32), axis=0).astype(jnp.bfloat16)


def solution(mesh):
    placed = (
        P("span", "head"),
        P(None, "head"),
        P(None, "head"),
        P("head", None),
        P("head"),
        P(None, "span"),
        P(None, "span"),
    )
    return jax.shard_map(
        shards, mesh=mesh, in_specs=placed, out_specs=P(("span", "head"), None), check_vma=False
    )
```

```python
import jax
import jax.numpy as jnp
from jax import lax
from jax.experimental import pallas as pl
from jax.experimental.pallas import tpu as pltpu
from jax.sharding import PartitionSpec as P

HEAD_DIM = 128
BLOCK = 128


epsilon = 1e-05


def passed_along(block, axis, distance):
    devices = range(lax.axis_size(axis))
    route = [((i - distance) % len(devices), i) for i in devices]
    return lax.ppermute(block, axis, route)


def layer_norm(embedding_activity):
    content_embeddings = embedding_activity.astype(jnp.float32)
    row_mean = jnp.mean(content_embeddings, axis=-1, keepdims=True)
    centred = content_embeddings - row_mean
    row_var = jnp.mean(centred * centred, axis=-1, keepdims=True)
    return (centred * lax.rsqrt(row_var + epsilon)).astype(jnp.bfloat16)


def block_attention_kernel(
    sharp_ref, order_ref, prior_ref, here_ref, shared_proj_ref, value_proj_ref, place_ref,
    back_ref, out_ref, total_ref,
):
    n_groups, n_rounds, rows_here, group_cols = here_ref.shape
    heads = out_ref.shape[2] // HEAD_DIM
    n_blocks = out_ref.shape[1] // BLOCK
    total_ref[...] = jnp.zeros_like(total_ref)
    features = n_groups * group_cols
    rows = lax.broadcasted_iota(jnp.int32, (BLOCK, 2 * BLOCK), 0)
    key_cols = lax.broadcasted_iota(jnp.int32, (BLOCK, 2 * BLOCK), 1)
    allowed = key_cols != rows + BLOCK
    for r in range(n_rounds):
        parts = [
            jnp.concatenate([prior_ref[order_ref[g], r], here_ref[g, r]], axis=0).astype(jnp.float32)
            for g in range(n_groups)
        ]
        row_mean = sum(jnp.sum(p, axis=1, keepdims=True) for p in parts) / features
        centred = [p - row_mean for p in parts]
        row_var = sum(jnp.sum(c * c, axis=1, keepdims=True) for c in centred) / features
        inv = lax.rsqrt(row_var + epsilon)
        normed = [(c * inv).astype(jnp.bfloat16) for c in centred]
        projected = []
        for proj_ref in (shared_proj_ref, value_proj_ref):
            acc = None
            for g in range(n_groups):
                term = jnp.dot(
                    normed[g],
                    proj_ref[group_cols * g : group_cols * (g + 1), :],
                    preferred_element_type=jnp.float32,
                )
                acc = term if acc is None else acc + term
            projected.append(acc.astype(jnp.bfloat16))
        shared, values_all = projected
        for h in range(heads):
            scale = sharp_ref[h]
            spread = shared[:, HEAD_DIM * h : HEAD_DIM * (h + 1)].astype(jnp.float32)
            unit = (
                spread * lax.rsqrt(jnp.sum(spread * spread, axis=1, keepdims=True) + 1e-06)
            ).astype(jnp.bfloat16)
            for b in range(n_blocks):
                queries = unit[BLOCK * (b + 1) : BLOCK * (b + 2)]
                keys = unit[BLOCK * b : BLOCK * (b + 2)]
                values = values_all[BLOCK * b : BLOCK * (b + 2), HEAD_DIM * h : HEAD_DIM * (h + 1)]
                scores = lax.dot_general(
                    queries, keys, (((1,), (1,)), ((), ())), preferred_element_type=jnp.float32
                ) * scale
                exp_scores = jnp.where(allowed, jnp.exp(scores), 0.0)
                totals = jnp.sum(exp_scores, axis=1, keepdims=True)
                weights = (exp_scores / totals).astype(jnp.bfloat16)
                mixed = jnp.dot(weights, values, preferred_element_type=jnp.float32)
                out_ref[r, BLOCK * b : BLOCK * (b + 1), HEAD_DIM * h : HEAD_DIM * (h + 1)] = (
                    mixed.astype(out_ref.dtype)
                )
                high = totals.astype(jnp.bfloat16)
                low = (totals - high.astype(jnp.float32)).astype(jnp.bfloat16)
                total_ref[r, BLOCK * b : BLOCK * (b + 1), h : h + 1] = high
                total_ref[r, BLOCK * b : BLOCK * (b + 1), heads + h : heads + h + 1] = low
    buffer_rows = back_ref.shape[0]
    cols = out_ref.shape[2]
    row_ids = lax.broadcasted_iota(jnp.int32, (buffer_rows, rows_here), 0)
    back_rows = None
    back_totals = None
    for r in range(n_rounds):
        hot = jnp.where(row_ids == place_ref[r : r + 1, :], 1.0, 0.0).astype(jnp.bfloat16)
        rows_part = jnp.dot(hot, out_ref[r], preferred_element_type=jnp.float32)
        totals_part = jnp.dot(hot, total_ref[r], preferred_element_type=jnp.float32)
        back_rows = rows_part if back_rows is None else back_rows + rows_part
        back_totals = totals_part if back_totals is None else back_totals + totals_part
    back_ref[:, :cols] = back_rows.astype(back_ref.dtype)
    back_ref[:, cols:] = back_totals[:, : back_ref.shape[1] - cols].astype(back_ref.dtype)


def block_attention(prior, order, here, shared_proj, value_proj, sharpness, place, buffer_rows):
    n_groups, n_rounds, rows_here, group_cols = here.shape
    span_rows = rows_here + BLOCK
    cols = shared_proj.shape[1]
    heads = cols // HEAD_DIM
    n_blocks = rows_here // BLOCK
    flops = n_rounds * heads * n_blocks * 4 * BLOCK * 2 * BLOCK * HEAD_DIM
    flops += n_rounds * span_rows * n_groups * group_cols * 2 * cols * 2
    flops += n_rounds * buffer_rows * rows_here * 2 * (cols + BLOCK)
    vmem = pl.BlockSpec(memory_space=pltpu.VMEM)
    smem = pl.BlockSpec(memory_space=pltpu.SMEM)
    back, _, _ = pl.pallas_call(
        block_attention_kernel,
        in_specs=[smem, smem, vmem, vmem, vmem, vmem, vmem],
        out_specs=[vmem, vmem, vmem],
        out_shape=[
            jax.ShapeDtypeStruct((buffer_rows, cols + 2 * heads), jnp.bfloat16),
            jax.ShapeDtypeStruct((n_rounds, rows_here, cols), jnp.bfloat16),
            jax.ShapeDtypeStruct((n_rounds, rows_here, BLOCK), jnp.bfloat16),
        ],
        cost_estimate=pl.CostEstimate(
            flops=flops,
            transcendentals=n_rounds * heads * n_blocks * BLOCK * 2 * BLOCK,
            bytes_accessed=(prior.size + here.size) * 2 + 4 * shared_proj.size
            + buffer_rows * (cols + 2 * heads) * 2,
        ),
    )(sharpness, order, prior, here, shared_proj, value_proj, place)
    return back


def rank_within_group(group, order):
    same = group[:, :, None] == group[:, None, :]
    earlier = order[:, None, :] < order[:, :, None]
    return jnp.sum((same & earlier).astype(jnp.int32), axis=2)


def one_hot_rows(index, count):
    return (index[:, :, None] == jnp.arange(count, dtype=jnp.int32)[None, None, :]).astype(
        jnp.bfloat16
    )


def shards(
    embedding_activity,
    common_lookup_projector,
    content_projector,
    final_projector,
    lane_sharpness,
    sorted_place_per_element,
    element_per_sorted_place,
):
    n_dev = lax.axis_size("span")
    rows_here = embedding_activity.shape[0]
    capacity = 2 * rows_here // n_dev
    n_rounds = sorted_place_per_element.shape[0]
    per_peer = n_rounds * capacity
    buffer_rows = n_dev * per_peer
    head_cols = common_lookup_projector.shape[1]
    heads_here = head_cols // HEAD_DIM
    blocks_here = rows_here // BLOCK
    round_ids = jnp.arange(n_rounds, dtype=jnp.int32)[:, None]
    local_ids = jnp.broadcast_to(
        jnp.arange(rows_here, dtype=jnp.int32)[None, :], (n_rounds, rows_here)
    )

    target = sorted_place_per_element // rows_here
    send_rank = rank_within_group(target, local_ids)
    send_row = target * per_peer + round_ids * capacity + send_rank
    send_hot = one_hot_rows(send_row, buffer_rows)

    source = element_per_sorted_place // rows_here
    within = element_per_sorted_place % rows_here
    recv_rank = rank_within_group(source, within)
    recv_row = source * per_peer + round_ids * capacity + recv_rank
    recv_hot = one_hot_rows(recv_row, buffer_rows)

    outgoing = jnp.einsum(
        "rtq,tf->qf", send_hot, embedding_activity, preferred_element_type=jnp.float32
    ).astype(jnp.bfloat16)
    incoming = lax.all_to_all(outgoing, "span", split_axis=0, concat_axis=0, tiled=True)
    arrived = jnp.einsum(
        "rsq,qf->rsf", recv_hot, incoming, preferred_element_type=jnp.float32
    ).astype(jnp.bfloat16)
    n_groups = lax.axis_size("head")
    copies = jnp.broadcast_to(arrived[None], (n_groups,) + arrived.shape)
    gathered = lax.all_to_all(copies, "head", split_axis=0, concat_axis=0, tiled=True)
    last_slice = arrived[:, rows_here - BLOCK :]
    received = []
    for shift in range(n_groups):
        route = [
            (s * n_groups + g, ((s + 1) % n_dev) * n_groups + (g + shift) % n_groups)
            for s in range(n_dev)
            for g in range(n_groups)
        ]
        received.append(lax.ppermute(last_slice, ("span", "head"), route))
    received, gathered = lax.optimization_barrier((received, gathered))
    group_here = lax.axis_index("head")
    slice_order = (group_here - jnp.arange(n_groups, dtype=jnp.int32)) % n_groups
    prior_stack = jnp.stack(received)
    back = block_attention(
        prior_stack,
        slice_order,
        gathered,
        common_lookup_projector,
        content_projector,
        lane_sharpness,
        recv_row,
        buffer_rows,
    )
    home = lax.all_to_all(back, "span", split_axis=0, concat_axis=0, tiled=True)
    token_all = jnp.einsum("rtq,qw->rtw", send_hot, home, preferred_element_type=jnp.float32)
    token_rows = token_all[:, :, :head_cols]
    token_totals = (
        token_all[:, :, head_cols : head_cols + heads_here]
        + token_all[:, :, head_cols + heads_here : head_cols + 2 * heads_here]
    )
    round_share = token_totals / jnp.sum(token_totals, axis=0)
    token_spread = token_rows.reshape(n_rounds, rows_here, heads_here, HEAD_DIM)
    combined = jnp.sum(round_share[..., None] * token_spread, axis=0).astype(jnp.bfloat16)
    combined = combined.reshape(rows_here, head_cols)
    group_part = jnp.dot(
        combined, final_projector, preferred_element_type=jnp.float32
    ).astype(jnp.bfloat16)
    group_parts = lax.all_to_all(
        group_part.reshape(n_groups, rows_here // n_groups, group_part.shape[1]),
        "head",
        split_axis=0,
        concat_axis=0,
        tiled=True,
    )
    return jnp.sum(group_parts.astype(jnp.float32), axis=0).astype(jnp.bfloat16)


def solution(mesh):
    placed = (
        P("span", "head"),
        P(None, "head"),
        P(None, "head"),
        P("head", None),
        P("head"),
        P(None, "span"),
        P(None, "span"),
    )
    return jax.shard_map(
        shards, mesh=mesh, in_specs=placed, out_specs=P(("span", "head"), None), check_vma=False
    )
```

```python
import jax
import jax.numpy as jnp
from jax import lax
from jax.experimental import pallas as pl
from jax.experimental.pallas import tpu as pltpu
from jax.sharding import PartitionSpec as P

HEAD_DIM = 128
BLOCK = 128


epsilon = 1e-05


def passed_along(block, axis, distance):
    devices = range(lax.axis_size(axis))
    route = [((i - distance) % len(devices), i) for i in devices]
    return lax.ppermute(block, axis, route)


def layer_norm(embedding_activity):
    content_embeddings = embedding_activity.astype(jnp.float32)
    row_mean = jnp.mean(content_embeddings, axis=-1, keepdims=True)
    centred = content_embeddings - row_mean
    row_var = jnp.mean(centred * centred, axis=-1, keepdims=True)
    return (centred * lax.rsqrt(row_var + epsilon)).astype(jnp.bfloat16)


def block_attention_kernel(sharp_ref, order_ref, *refs):
    n_groups = len(refs) - 7
    prior_refs = refs[:n_groups]
    here_ref, shared_proj_ref, value_proj_ref, place_ref, back_ref, out_ref, total_ref = refs[
        n_groups:
    ]
    n_groups, n_rounds, rows_here, group_cols = here_ref.shape
    heads = out_ref.shape[2] // HEAD_DIM
    n_blocks = out_ref.shape[1] // BLOCK
    total_ref[...] = jnp.zeros_like(total_ref)
    features = n_groups * group_cols
    rows = lax.broadcasted_iota(jnp.int32, (BLOCK, 2 * BLOCK), 0)
    key_cols = lax.broadcasted_iota(jnp.int32, (BLOCK, 2 * BLOCK), 1)
    allowed = key_cols != rows + BLOCK
    for r in range(n_rounds):
        parts = []
        for g in range(n_groups):
            prior = prior_refs[0][r]
            for k in range(1, n_groups):
                prior = jnp.where(order_ref[g] == k, prior_refs[k][r], prior)
            parts.append(
                jnp.concatenate([prior, here_ref[g, r]], axis=0).astype(jnp.float32)
            )
        row_mean = sum(jnp.sum(p, axis=1, keepdims=True) for p in parts) / features
        centred = [p - row_mean for p in parts]
        row_var = sum(jnp.sum(c * c, axis=1, keepdims=True) for c in centred) / features
        inv = lax.rsqrt(row_var + epsilon)
        normed = [(c * inv).astype(jnp.bfloat16) for c in centred]
        projected = []
        for proj_ref in (shared_proj_ref, value_proj_ref):
            acc = None
            for g in range(n_groups):
                term = jnp.dot(
                    normed[g],
                    proj_ref[group_cols * g : group_cols * (g + 1), :],
                    preferred_element_type=jnp.float32,
                )
                acc = term if acc is None else acc + term
            projected.append(acc.astype(jnp.bfloat16))
        shared, values_all = projected
        for h in range(heads):
            scale = sharp_ref[h]
            spread = shared[:, HEAD_DIM * h : HEAD_DIM * (h + 1)].astype(jnp.float32)
            unit = (
                spread * lax.rsqrt(jnp.sum(spread * spread, axis=1, keepdims=True) + 1e-06)
            ).astype(jnp.bfloat16)
            for b in range(n_blocks):
                queries = unit[BLOCK * (b + 1) : BLOCK * (b + 2)]
                keys = unit[BLOCK * b : BLOCK * (b + 2)]
                values = values_all[BLOCK * b : BLOCK * (b + 2), HEAD_DIM * h : HEAD_DIM * (h + 1)]
                scores = lax.dot_general(
                    queries, keys, (((1,), (1,)), ((), ())), preferred_element_type=jnp.float32
                ) * scale
                exp_scores = jnp.where(allowed, jnp.exp(scores), 0.0)
                totals = jnp.sum(exp_scores, axis=1, keepdims=True)
                weights = (exp_scores / totals).astype(jnp.bfloat16)
                mixed = jnp.dot(weights, values, preferred_element_type=jnp.float32)
                out_ref[r, BLOCK * b : BLOCK * (b + 1), HEAD_DIM * h : HEAD_DIM * (h + 1)] = (
                    mixed.astype(out_ref.dtype)
                )
                high = totals.astype(jnp.bfloat16)
                low = (totals - high.astype(jnp.float32)).astype(jnp.bfloat16)
                total_ref[r, BLOCK * b : BLOCK * (b + 1), h : h + 1] = high
                total_ref[r, BLOCK * b : BLOCK * (b + 1), heads + h : heads + h + 1] = low
    buffer_rows = back_ref.shape[0]
    cols = out_ref.shape[2]
    row_ids = lax.broadcasted_iota(jnp.int32, (buffer_rows, rows_here), 0)
    back_rows = None
    back_totals = None
    for r in range(n_rounds):
        hot = jnp.where(row_ids == place_ref[r : r + 1, :], 1.0, 0.0).astype(jnp.bfloat16)
        rows_part = jnp.dot(hot, out_ref[r], preferred_element_type=jnp.float32)
        totals_part = jnp.dot(hot, total_ref[r], preferred_element_type=jnp.float32)
        back_rows = rows_part if back_rows is None else back_rows + rows_part
        back_totals = totals_part if back_totals is None else back_totals + totals_part
    back_ref[:, :cols] = back_rows.astype(back_ref.dtype)
    back_ref[:, cols:] = back_totals[:, : back_ref.shape[1] - cols].astype(back_ref.dtype)


def block_attention(prior, order, here, shared_proj, value_proj, sharpness, place, buffer_rows):
    n_groups, n_rounds, rows_here, group_cols = here.shape
    span_rows = rows_here + BLOCK
    cols = shared_proj.shape[1]
    heads = cols // HEAD_DIM
    n_blocks = rows_here // BLOCK
    flops = n_rounds * heads * n_blocks * 4 * BLOCK * 2 * BLOCK * HEAD_DIM
    flops += n_rounds * span_rows * n_groups * group_cols * 2 * cols * 2
    flops += n_rounds * buffer_rows * rows_here * 2 * (cols + BLOCK)
    vmem = pl.BlockSpec(memory_space=pltpu.VMEM)
    smem = pl.BlockSpec(memory_space=pltpu.SMEM)
    back, _, _ = pl.pallas_call(
        block_attention_kernel,
        in_specs=[smem, smem] + [vmem] * (len(prior) + 4),
        out_specs=[vmem, vmem, vmem],
        out_shape=[
            jax.ShapeDtypeStruct((buffer_rows, cols + 2 * heads), jnp.bfloat16),
            jax.ShapeDtypeStruct((n_rounds, rows_here, cols), jnp.bfloat16),
            jax.ShapeDtypeStruct((n_rounds, rows_here, BLOCK), jnp.bfloat16),
        ],
        cost_estimate=pl.CostEstimate(
            flops=flops,
            transcendentals=n_rounds * heads * n_blocks * BLOCK * 2 * BLOCK,
            bytes_accessed=(sum(p.size for p in prior) + here.size) * 2 + 4 * shared_proj.size
            + buffer_rows * (cols + 2 * heads) * 2,
        ),
    )(sharpness, order, *prior, here, shared_proj, value_proj, place)
    return back


def rank_within_group(group, order):
    same = group[:, :, None] == group[:, None, :]
    earlier = order[:, None, :] < order[:, :, None]
    return jnp.sum((same & earlier).astype(jnp.int32), axis=2)


def one_hot_rows(index, count):
    return (index[:, :, None] == jnp.arange(count, dtype=jnp.int32)[None, None, :]).astype(
        jnp.bfloat16
    )


def shards(
    embedding_activity,
    common_lookup_projector,
    content_projector,
    final_projector,
    lane_sharpness,
    sorted_place_per_element,
    element_per_sorted_place,
):
    n_dev = lax.axis_size("span")
    rows_here = embedding_activity.shape[0]
    capacity = 2 * rows_here // n_dev
    n_rounds = sorted_place_per_element.shape[0]
    per_peer = n_rounds * capacity
    buffer_rows = n_dev * per_peer
    head_cols = common_lookup_projector.shape[1]
    heads_here = head_cols // HEAD_DIM
    blocks_here = rows_here // BLOCK
    round_ids = jnp.arange(n_rounds, dtype=jnp.int32)[:, None]
    local_ids = jnp.broadcast_to(
        jnp.arange(rows_here, dtype=jnp.int32)[None, :], (n_rounds, rows_here)
    )

    target = sorted_place_per_element // rows_here
    send_rank = rank_within_group(target, local_ids)
    send_row = target * per_peer + round_ids * capacity + send_rank
    send_hot = one_hot_rows(send_row, buffer_rows)

    source = element_per_sorted_place // rows_here
    within = element_per_sorted_place % rows_here
    recv_rank = rank_within_group(source, within)
    recv_row = source * per_peer + round_ids * capacity + recv_rank
    recv_hot = one_hot_rows(recv_row, buffer_rows)

    outgoing = jnp.einsum(
        "rtq,tf->qf", send_hot, embedding_activity, preferred_element_type=jnp.float32
    ).astype(jnp.bfloat16)
    incoming = lax.all_to_all(outgoing, "span", split_axis=0, concat_axis=0, tiled=True)
    arrived = jnp.einsum(
        "rsq,qf->rsf", recv_hot, incoming, preferred_element_type=jnp.float32
    ).astype(jnp.bfloat16)
    n_groups = lax.axis_size("head")
    copies = jnp.broadcast_to(arrived[None], (n_groups,) + arrived.shape)
    gathered = lax.all_to_all(copies, "head", split_axis=0, concat_axis=0, tiled=True)
    last_slice = arrived[:, rows_here - BLOCK :]
    received = []
    for shift in range(n_groups):
        route = [
            (s * n_groups + g, ((s + 1) % n_dev) * n_groups + (g + shift) % n_groups)
            for s in range(n_dev)
            for g in range(n_groups)
        ]
        received.append(lax.ppermute(last_slice, ("span", "head"), route))
    received, gathered = lax.optimization_barrier((received, gathered))
    group_here = lax.axis_index("head")
    slice_order = (group_here - jnp.arange(n_groups, dtype=jnp.int32)) % n_groups
    back = block_attention(
        list(received),
        slice_order,
        gathered,
        common_lookup_projector,
        content_projector,
        lane_sharpness,
        recv_row,
        buffer_rows,
    )
    home = lax.all_to_all(back, "span", split_axis=0, concat_axis=0, tiled=True)
    token_all = jnp.einsum("rtq,qw->rtw", send_hot, home, preferred_element_type=jnp.float32)
    token_rows = token_all[:, :, :head_cols]
    token_totals = (
        token_all[:, :, head_cols : head_cols + heads_here]
        + token_all[:, :, head_cols + heads_here : head_cols + 2 * heads_here]
    )
    round_share = token_totals / jnp.sum(token_totals, axis=0)
    token_spread = token_rows.reshape(n_rounds, rows_here, heads_here, HEAD_DIM)
    combined = jnp.sum(round_share[..., None] * token_spread, axis=0).astype(jnp.bfloat16)
    combined = combined.reshape(rows_here, head_cols)
    group_part = jnp.dot(
        combined, final_projector, preferred_element_type=jnp.float32
    ).astype(jnp.bfloat16)
    group_parts = lax.all_to_all(
        group_part.reshape(n_groups, rows_here // n_groups, group_part.shape[1]),
        "head",
        split_axis=0,
        concat_axis=0,
        tiled=True,
    )
    return jnp.sum(group_parts.astype(jnp.float32), axis=0).astype(jnp.bfloat16)


def solution(mesh):
    placed = (
        P("span", "head"),
        P(None, "head"),
        P(None, "head"),
        P("head", None),
        P("head"),
        P(None, "span"),
        P(None, "span"),
    )
    return jax.shard_map(
        shards, mesh=mesh, in_specs=placed, out_specs=P(("span", "head"), None), check_vma=False
    )
```

```python
import jax
import jax.numpy as jnp
from jax import lax
from jax.experimental import pallas as pl
from jax.experimental.pallas import tpu as pltpu
from jax.sharding import PartitionSpec as P

HEAD_DIM = 128
BLOCK = 128


epsilon = 1e-05


def passed_along(block, axis, distance):
    devices = range(lax.axis_size(axis))
    route = [((i - distance) % len(devices), i) for i in devices]
    return lax.ppermute(block, axis, route)


def layer_norm(embedding_activity):
    content_embeddings = embedding_activity.astype(jnp.float32)
    row_mean = jnp.mean(content_embeddings, axis=-1, keepdims=True)
    centred = content_embeddings - row_mean
    row_var = jnp.mean(centred * centred, axis=-1, keepdims=True)
    return (centred * lax.rsqrt(row_var + epsilon)).astype(jnp.bfloat16)


def block_attention_kernel(
    sharp_ref, order_ref, prior_ref, here_ref, shared_proj_ref, value_proj_ref, place_ref,
    back_ref, out_ref, total_ref,
):
    n_groups, n_rounds, rows_here, group_cols = here_ref.shape
    heads = out_ref.shape[2] // HEAD_DIM
    n_blocks = out_ref.shape[1] // BLOCK
    total_ref[...] = jnp.zeros_like(total_ref)
    features = n_groups * group_cols
    rows = lax.broadcasted_iota(jnp.int32, (BLOCK, 2 * BLOCK), 0)
    key_cols = lax.broadcasted_iota(jnp.int32, (BLOCK, 2 * BLOCK), 1)
    allowed = key_cols != rows + BLOCK
    for r in range(n_rounds):
        parts = [
            jnp.concatenate([prior_ref[order_ref[g], r], here_ref[g, r]], axis=0).astype(jnp.float32)
            for g in range(n_groups)
        ]
        row_mean = sum(jnp.sum(p, axis=1, keepdims=True) for p in parts) / features
        centred = [p - row_mean for p in parts]
        row_var = sum(jnp.sum(c * c, axis=1, keepdims=True) for c in centred) / features
        inv = lax.rsqrt(row_var + epsilon)
        normed = [(c * inv).astype(jnp.bfloat16) for c in centred]
        projected = []
        for proj_ref in (shared_proj_ref, value_proj_ref):
            acc = None
            for g in range(n_groups):
                term = jnp.dot(
                    normed[g],
                    proj_ref[group_cols * g : group_cols * (g + 1), :],
                    preferred_element_type=jnp.float32,
                )
                acc = term if acc is None else acc + term
            projected.append(acc.astype(jnp.bfloat16))
        shared, values_all = projected
        for h in range(heads):
            scale = sharp_ref[h]
            spread = shared[:, HEAD_DIM * h : HEAD_DIM * (h + 1)].astype(jnp.float32)
            unit = (
                spread * lax.rsqrt(jnp.sum(spread * spread, axis=1, keepdims=True) + 1e-06)
            ).astype(jnp.bfloat16)
            for b in range(n_blocks):
                queries = unit[BLOCK * (b + 1) : BLOCK * (b + 2)]
                keys = unit[BLOCK * b : BLOCK * (b + 2)]
                values = values_all[BLOCK * b : BLOCK * (b + 2), HEAD_DIM * h : HEAD_DIM * (h + 1)]
                scores = lax.dot_general(
                    queries, keys, (((1,), (1,)), ((), ())), preferred_element_type=jnp.float32
                ) * scale
                exp_scores = jnp.where(allowed, jnp.exp(scores), 0.0)
                totals = jnp.sum(exp_scores, axis=1, keepdims=True)
                weights = (exp_scores / totals).astype(jnp.bfloat16)
                mixed = jnp.dot(weights, values, preferred_element_type=jnp.float32)
                out_ref[r, BLOCK * b : BLOCK * (b + 1), HEAD_DIM * h : HEAD_DIM * (h + 1)] = (
                    mixed.astype(out_ref.dtype)
                )
                high = totals.astype(jnp.bfloat16)
                low = (totals - high.astype(jnp.float32)).astype(jnp.bfloat16)
                total_ref[r, BLOCK * b : BLOCK * (b + 1), h : h + 1] = high
                total_ref[r, BLOCK * b : BLOCK * (b + 1), heads + h : heads + h + 1] = low
    buffer_rows = back_ref.shape[0]
    cols = out_ref.shape[2]
    row_ids = lax.broadcasted_iota(jnp.int32, (buffer_rows, rows_here), 0)
    back_rows = None
    back_totals = None
    for r in range(n_rounds):
        hot = jnp.where(row_ids == place_ref[r : r + 1, :], 1.0, 0.0).astype(jnp.bfloat16)
        rows_part = jnp.dot(hot, out_ref[r], preferred_element_type=jnp.float32)
        totals_part = jnp.dot(hot, total_ref[r], preferred_element_type=jnp.float32)
        back_rows = rows_part if back_rows is None else back_rows + rows_part
        back_totals = totals_part if back_totals is None else back_totals + totals_part
    back_ref[:, :cols] = back_rows.astype(back_ref.dtype)
    back_ref[:, cols:] = back_totals[:, : back_ref.shape[1] - cols].astype(back_ref.dtype)


def block_attention(prior, order, here, shared_proj, value_proj, sharpness, place, buffer_rows):
    n_groups, n_rounds, rows_here, group_cols = here.shape
    span_rows = rows_here + BLOCK
    cols = shared_proj.shape[1]
    heads = cols // HEAD_DIM
    n_blocks = rows_here // BLOCK
    flops = n_rounds * heads * n_blocks * 4 * BLOCK * 2 * BLOCK * HEAD_DIM
    flops += n_rounds * span_rows * n_groups * group_cols * 2 * cols * 2
    flops += n_rounds * buffer_rows * rows_here * 2 * (cols + BLOCK)
    vmem = pl.BlockSpec(memory_space=pltpu.VMEM)
    smem = pl.BlockSpec(memory_space=pltpu.SMEM)
    back, _, _ = pl.pallas_call(
        block_attention_kernel,
        in_specs=[smem, smem, vmem, vmem, vmem, vmem, vmem],
        out_specs=[vmem, vmem, vmem],
        out_shape=[
            jax.ShapeDtypeStruct((buffer_rows, cols + 2 * heads), jnp.bfloat16),
            jax.ShapeDtypeStruct((n_rounds, rows_here, cols), jnp.bfloat16),
            jax.ShapeDtypeStruct((n_rounds, rows_here, BLOCK), jnp.bfloat16),
        ],
        cost_estimate=pl.CostEstimate(
            flops=flops,
            transcendentals=n_rounds * heads * n_blocks * BLOCK * 2 * BLOCK,
            bytes_accessed=(prior.size + here.size) * 2 + 4 * shared_proj.size
            + buffer_rows * (cols + 2 * heads) * 2,
        ),
    )(sharpness, order, prior, here, shared_proj, value_proj, place)
    return back


def rank_within_group(group, order):
    same = group[:, :, None] == group[:, None, :]
    earlier = order[:, None, :] < order[:, :, None]
    return jnp.sum((same & earlier).astype(jnp.int32), axis=2)


def one_hot_rows(index, count):
    return (index[:, :, None] == jnp.arange(count, dtype=jnp.int32)[None, None, :]).astype(
        jnp.bfloat16
    )


def shards(
    embedding_activity,
    common_lookup_projector,
    content_projector,
    final_projector,
    lane_sharpness,
    sorted_place_per_element,
    element_per_sorted_place,
):
    n_dev = lax.axis_size("span")
    rows_here = embedding_activity.shape[0]
    capacity = 2 * rows_here // n_dev
    n_rounds = sorted_place_per_element.shape[0]
    per_peer = n_rounds * capacity
    buffer_rows = n_dev * per_peer
    head_cols = common_lookup_projector.shape[1]
    heads_here = head_cols // HEAD_DIM
    blocks_here = rows_here // BLOCK
    round_ids = jnp.arange(n_rounds, dtype=jnp.int32)[:, None]
    local_ids = jnp.broadcast_to(
        jnp.arange(rows_here, dtype=jnp.int32)[None, :], (n_rounds, rows_here)
    )

    target = sorted_place_per_element // rows_here

    source = element_per_sorted_place // rows_here
    within = element_per_sorted_place % rows_here

    ranks = rank_within_group(
        jnp.concatenate([target, source], axis=0), jnp.concatenate([local_ids, within], axis=0)
    )
    send_rank, recv_rank = ranks[:n_rounds], ranks[n_rounds:]
    send_row = target * per_peer + round_ids * capacity + send_rank
    send_hot = one_hot_rows(send_row, buffer_rows)
    recv_row = source * per_peer + round_ids * capacity + recv_rank
    recv_hot = one_hot_rows(recv_row, buffer_rows)

    outgoing = jnp.einsum(
        "rtq,tf->qf", send_hot, embedding_activity, preferred_element_type=jnp.float32
    ).astype(jnp.bfloat16)
    incoming = lax.all_to_all(outgoing, "span", split_axis=0, concat_axis=0, tiled=True)
    arrived = jnp.einsum(
        "rsq,qf->rsf", recv_hot, incoming, preferred_element_type=jnp.float32
    ).astype(jnp.bfloat16)
    n_groups = lax.axis_size("head")
    copies = jnp.broadcast_to(arrived[None], (n_groups,) + arrived.shape)
    gathered = lax.all_to_all(copies, "head", split_axis=0, concat_axis=0, tiled=True)
    last_slice = arrived[:, rows_here - BLOCK :]
    received = []
    for shift in range(n_groups):
        route = [
            (s * n_groups + g, ((s + 1) % n_dev) * n_groups + (g + shift) % n_groups)
            for s in range(n_dev)
            for g in range(n_groups)
        ]
        received.append(lax.ppermute(last_slice, ("span", "head"), route))
    received, gathered = lax.optimization_barrier((received, gathered))
    group_here = lax.axis_index("head")
    slice_order = (group_here - jnp.arange(n_groups, dtype=jnp.int32)) % n_groups
    prior_stack = jnp.stack(received)
    back = block_attention(
        prior_stack,
        slice_order,
        gathered,
        common_lookup_projector,
        content_projector,
        lane_sharpness,
        recv_row,
        buffer_rows,
    )
    home = lax.all_to_all(back, "span", split_axis=0, concat_axis=0, tiled=True)
    token_all = jnp.einsum("rtq,qw->rtw", send_hot, home, preferred_element_type=jnp.float32)
    token_rows = token_all[:, :, :head_cols]
    token_totals = (
        token_all[:, :, head_cols : head_cols + heads_here]
        + token_all[:, :, head_cols + heads_here : head_cols + 2 * heads_here]
    )
    round_share = token_totals / jnp.sum(token_totals, axis=0)
    token_spread = token_rows.reshape(n_rounds, rows_here, heads_here, HEAD_DIM)
    combined = jnp.sum(round_share[..., None] * token_spread, axis=0).astype(jnp.bfloat16)
    combined = combined.reshape(rows_here, head_cols)
    group_part = jnp.dot(
        combined, final_projector, preferred_element_type=jnp.float32
    ).astype(jnp.bfloat16)
    group_parts = lax.all_to_all(
        group_part.reshape(n_groups, rows_here // n_groups, group_part.shape[1]),
        "head",
        split_axis=0,
        concat_axis=0,
        tiled=True,
    )
    return jnp.sum(group_parts.astype(jnp.float32), axis=0).astype(jnp.bfloat16)


def solution(mesh):
    placed = (
        P("span", "head"),
        P(None, "head"),
        P(None, "head"),
        P("head", None),
        P("head"),
        P(None, "span"),
        P(None, "span"),
    )
    return jax.shard_map(
        shards, mesh=mesh, in_specs=placed, out_specs=P(("span", "head"), None), check_vma=False
    )
```

```python
import jax
import jax.numpy as jnp
from jax import lax
from jax.experimental import pallas as pl
from jax.experimental.pallas import tpu as pltpu
from jax.sharding import PartitionSpec as P

HEAD_DIM = 128
BLOCK = 128


epsilon = 1e-05


def passed_along(block, axis, distance):
    devices = range(lax.axis_size(axis))
    route = [((i - distance) % len(devices), i) for i in devices]
    return lax.ppermute(block, axis, route)


def layer_norm(embedding_activity):
    content_embeddings = embedding_activity.astype(jnp.float32)
    row_mean = jnp.mean(content_embeddings, axis=-1, keepdims=True)
    centred = content_embeddings - row_mean
    row_var = jnp.mean(centred * centred, axis=-1, keepdims=True)
    return (centred * lax.rsqrt(row_var + epsilon)).astype(jnp.bfloat16)


def block_attention_kernel(
    sharp_ref, order_ref, prior_ref, here_ref, shared_proj_ref, value_proj_ref, place_ref,
    back_ref, out_ref, total_ref,
):
    n_groups, n_rounds, rows_here, group_cols = here_ref.shape
    heads = out_ref.shape[2] // HEAD_DIM
    n_blocks = out_ref.shape[1] // BLOCK
    total_ref[...] = jnp.zeros_like(total_ref)
    features = n_groups * group_cols
    rows = lax.broadcasted_iota(jnp.int32, (BLOCK, 2 * BLOCK), 0)
    key_cols = lax.broadcasted_iota(jnp.int32, (BLOCK, 2 * BLOCK), 1)
    allowed = key_cols != rows + BLOCK
    for r in range(n_rounds):
        parts = [
            jnp.concatenate([prior_ref[order_ref[g], r], here_ref[g, r]], axis=0).astype(jnp.float32)
            for g in range(n_groups)
        ]
        row_mean = sum(jnp.sum(p, axis=1, keepdims=True) for p in parts) / features
        centred = [p - row_mean for p in parts]
        row_var = sum(jnp.sum(c * c, axis=1, keepdims=True) for c in centred) / features
        inv = lax.rsqrt(row_var + epsilon)
        normed = [(c * inv).astype(jnp.bfloat16) for c in centred]
        projected = []
        for proj_ref in (shared_proj_ref, value_proj_ref):
            acc = None
            for g in range(n_groups):
                term = jnp.dot(
                    normed[g],
                    proj_ref[group_cols * g : group_cols * (g + 1), :],
                    preferred_element_type=jnp.float32,
                )
                acc = term if acc is None else acc + term
            projected.append(acc.astype(jnp.bfloat16))
        shared, values_all = projected
        for h in range(heads):
            scale = sharp_ref[h]
            spread = shared[:, HEAD_DIM * h : HEAD_DIM * (h + 1)].astype(jnp.float32)
            unit = (
                spread * lax.rsqrt(jnp.sum(spread * spread, axis=1, keepdims=True) + 1e-06)
            ).astype(jnp.bfloat16)
            for b in range(n_blocks):
                queries = unit[BLOCK * (b + 1) : BLOCK * (b + 2)]
                keys = unit[BLOCK * b : BLOCK * (b + 2)]
                values = values_all[BLOCK * b : BLOCK * (b + 2), HEAD_DIM * h : HEAD_DIM * (h + 1)]
                scores = lax.dot_general(
                    queries, keys, (((1,), (1,)), ((), ())), preferred_element_type=jnp.float32
                ) * scale
                exp_scores = jnp.where(allowed, jnp.exp(scores), 0.0)
                totals = jnp.sum(exp_scores, axis=1, keepdims=True)
                weights = (exp_scores / totals).astype(jnp.bfloat16)
                mixed = jnp.dot(weights, values, preferred_element_type=jnp.float32)
                out_ref[r, BLOCK * b : BLOCK * (b + 1), HEAD_DIM * h : HEAD_DIM * (h + 1)] = (
                    mixed.astype(out_ref.dtype)
                )
                high = totals.astype(jnp.bfloat16)
                low = (totals - high.astype(jnp.float32)).astype(jnp.bfloat16)
                total_ref[r, BLOCK * b : BLOCK * (b + 1), h : h + 1] = high
                total_ref[r, BLOCK * b : BLOCK * (b + 1), heads + h : heads + h + 1] = low
    buffer_rows = back_ref.shape[0]
    cols = out_ref.shape[2]
    row_ids = lax.broadcasted_iota(jnp.int32, (buffer_rows, rows_here), 0)
    back_rows = None
    back_totals = None
    for r in range(n_rounds):
        hot = jnp.where(row_ids == place_ref[r : r + 1, :], 1.0, 0.0).astype(jnp.bfloat16)
        rows_part = jnp.dot(hot, out_ref[r], preferred_element_type=jnp.float32)
        totals_part = jnp.dot(hot, total_ref[r], preferred_element_type=jnp.float32)
        back_rows = rows_part if back_rows is None else back_rows + rows_part
        back_totals = totals_part if back_totals is None else back_totals + totals_part
    back_ref[:, :cols] = back_rows.astype(back_ref.dtype)
    back_ref[:, cols:] = back_totals[:, : back_ref.shape[1] - cols].astype(back_ref.dtype)


def block_attention(prior, order, here, shared_proj, value_proj, sharpness, place, buffer_rows):
    n_groups, n_rounds, rows_here, group_cols = here.shape
    span_rows = rows_here + BLOCK
    cols = shared_proj.shape[1]
    heads = cols // HEAD_DIM
    n_blocks = rows_here // BLOCK
    flops = n_rounds * heads * n_blocks * 4 * BLOCK * 2 * BLOCK * HEAD_DIM
    flops += n_rounds * span_rows * n_groups * group_cols * 2 * cols * 2
    flops += n_rounds * buffer_rows * rows_here * 2 * (cols + BLOCK)
    vmem = pl.BlockSpec(memory_space=pltpu.VMEM)
    smem = pl.BlockSpec(memory_space=pltpu.SMEM)
    back, _, _ = pl.pallas_call(
        block_attention_kernel,
        in_specs=[smem, smem, vmem, vmem, vmem, vmem, vmem],
        out_specs=[vmem, vmem, vmem],
        out_shape=[
            jax.ShapeDtypeStruct((buffer_rows, cols + 2 * heads), jnp.bfloat16),
            jax.ShapeDtypeStruct((n_rounds, rows_here, cols), jnp.bfloat16),
            jax.ShapeDtypeStruct((n_rounds, rows_here, BLOCK), jnp.bfloat16),
        ],
        cost_estimate=pl.CostEstimate(
            flops=flops,
            transcendentals=n_rounds * heads * n_blocks * BLOCK * 2 * BLOCK,
            bytes_accessed=(prior.size + here.size) * 2 + 4 * shared_proj.size
            + buffer_rows * (cols + 2 * heads) * 2,
        ),
    )(sharpness, order, prior, here, shared_proj, value_proj, place)
    return back


def rank_within_group(group, order):
    same = group[:, :, None] == group[:, None, :]
    earlier = order[:, None, :] < order[:, :, None]
    return jnp.sum((same & earlier).astype(jnp.int32), axis=2)


def one_hot_rows(index, count):
    return (index[:, :, None] == jnp.arange(count, dtype=jnp.int32)[None, None, :]).astype(
        jnp.bfloat16
    )


def shards(
    embedding_activity,
    common_lookup_projector,
    content_projector,
    final_projector,
    lane_sharpness,
    sorted_place_per_element,
    element_per_sorted_place,
):
    n_dev = lax.axis_size("span")
    rows_here = embedding_activity.shape[0]
    capacity = 2 * rows_here // n_dev
    n_rounds = sorted_place_per_element.shape[0]
    per_peer = n_rounds * capacity
    buffer_rows = n_dev * per_peer
    head_cols = common_lookup_projector.shape[1]
    heads_here = head_cols // HEAD_DIM
    blocks_here = rows_here // BLOCK
    round_ids = jnp.arange(n_rounds, dtype=jnp.int32)[:, None]
    local_ids = jnp.broadcast_to(
        jnp.arange(rows_here, dtype=jnp.int32)[None, :], (n_rounds, rows_here)
    )

    target = sorted_place_per_element // rows_here
    send_rank = rank_within_group(target, local_ids)
    send_row = target * per_peer + round_ids * capacity + send_rank
    send_hot = one_hot_rows(send_row, buffer_rows)

    source = element_per_sorted_place // rows_here
    within = element_per_sorted_place % rows_here
    recv_rank = rank_within_group(source, within)
    recv_row = source * per_peer + round_ids * capacity + recv_rank
    recv_hot = one_hot_rows(recv_row, buffer_rows)

    outgoing = jnp.einsum(
        "rtq,tf->qf", send_hot, embedding_activity, preferred_element_type=jnp.float32
    ).astype(jnp.bfloat16)
    incoming = lax.all_to_all(outgoing, "span", split_axis=0, concat_axis=0, tiled=True)
    arrived = jnp.einsum(
        "rsq,qf->rsf", recv_hot, incoming, preferred_element_type=jnp.float32
    ).astype(jnp.bfloat16)
    n_groups = lax.axis_size("head")
    copies = jnp.einsum(
        "grsq,qf->grsf",
        jnp.broadcast_to(recv_hot[None], (n_groups,) + recv_hot.shape),
        incoming,
        preferred_element_type=jnp.float32,
    ).astype(jnp.bfloat16)
    gathered = lax.all_to_all(copies, "head", split_axis=0, concat_axis=0, tiled=True)
    last_slice = arrived[:, rows_here - BLOCK :]
    received = []
    for shift in range(n_groups):
        route = [
            (s * n_groups + g, ((s + 1) % n_dev) * n_groups + (g + shift) % n_groups)
            for s in range(n_dev)
            for g in range(n_groups)
        ]
        received.append(lax.ppermute(last_slice, ("span", "head"), route))
    received, gathered = lax.optimization_barrier((received, gathered))
    group_here = lax.axis_index("head")
    slice_order = (group_here - jnp.arange(n_groups, dtype=jnp.int32)) % n_groups
    prior_stack = jnp.stack(received)
    back = block_attention(
        prior_stack,
        slice_order,
        gathered,
        common_lookup_projector,
        content_projector,
        lane_sharpness,
        recv_row,
        buffer_rows,
    )
    home = lax.all_to_all(back, "span", split_axis=0, concat_axis=0, tiled=True)
    token_all = jnp.einsum("rtq,qw->rtw", send_hot, home, preferred_element_type=jnp.float32)
    token_rows = token_all[:, :, :head_cols]
    token_totals = (
        token_all[:, :, head_cols : head_cols + heads_here]
        + token_all[:, :, head_cols + heads_here : head_cols + 2 * heads_here]
    )
    round_share = token_totals / jnp.sum(token_totals, axis=0)
    token_spread = token_rows.reshape(n_rounds, rows_here, heads_here, HEAD_DIM)
    combined = jnp.sum(round_share[..., None] * token_spread, axis=0).astype(jnp.bfloat16)
    combined = combined.reshape(rows_here, head_cols)
    group_part = jnp.dot(
        combined, final_projector, preferred_element_type=jnp.float32
    ).astype(jnp.bfloat16)
    group_parts = lax.all_to_all(
        group_part.reshape(n_groups, rows_here // n_groups, group_part.shape[1]),
        "head",
        split_axis=0,
        concat_axis=0,
        tiled=True,
    )
    return jnp.sum(group_parts.astype(jnp.float32), axis=0).astype(jnp.bfloat16)


def solution(mesh):
    placed = (
        P("span", "head"),
        P(None, "head"),
        P(None, "head"),
        P("head", None),
        P("head"),
        P(None, "span"),
        P(None, "span"),
    )
    return jax.shard_map(
        shards, mesh=mesh, in_specs=placed, out_specs=P(("span", "head"), None), check_vma=False
    )
```
